512 devices in a mesh: dp: 16 (over x, y_lo, core), ctx: 32 (over z, y_hi).
Axes of the slice: x: 4, y: 4 (y_hi: 2, y_lo: 2; y = y_hi * 2 + y_lo), z: 16, core: 2. Of those that a mesh axis runs over, the one named last changes fastest.
Arguments:
- query: bfloat16 [512, 2, 64, 4096], P(('dp', 'ctx')), may hold values from -8 to 8
- keys: bfloat16 [512, 2, 64, 512], P(('dp', 'ctx')), may hold values from -8 to 8
- values: bfloat16 [512, 2, 64, 512], P(('dp', 'ctx')), may hold values from -6 to 6
- grad_out: bfloat16 [512, 2, 64, 4096], P(('dp', 'ctx')), may hold values from -6 to 6
- lengths: int32 [512], replicated, may hold values from 1 to 192, 65536 in all
Outputs:
- grad_query: bfloat16 [512, 2, 64, 4096], P(('dp', 'ctx'))
- grad_keys: bfloat16 [512, 2, 64, 512], P(('dp', 'ctx'))
- grad_values: bfloat16 [512, 2, 64, 512], P(('dp', 'ctx'))
The draws below stay inside these ranges and needn't reach their ends.
Inputs may be any that keep to these rules, and one draw needn't show every extreme that they name: lengths sum to 65536, and the largest is 192.
All inputs are finite; a program needn't handle non-finite values.
Results may differ from the reference program's by a relative error of at most 0.025.
Values may be sent and summed in bfloat16 or wider, within the bound.
No kernel may reach another device: no remote copies, remote signals or barrier semaphores. Data moves between devices by JAX's collectives and lax.ppermute only.
A program may use at most 64 MiB of HBM per device.

```python
import math
import jax
import jax.numpy as jnp
import numpy as np
from jax import lax

HEAD = 128
GROUP = 8
KV_HEADS = 4
HALF = 64
SHARDS = 512
LEN = 65536
NDOC = 512
DOC_MOST = 192


def paired_draw(key):
    base_key = jax.random.fold_in(key, 7)
    key_one, key_two = jax.random.split(base_key, 2)
    shape_query = (SHARDS, 2, HALF, KV_HEADS * GROUP * HEAD)
    shape_keys = (SHARDS, 2, HALF, KV_HEADS * HEAD)
    keys_out = jnp.clip(jax.random.normal(key_one, shape_keys, jnp.float32), -4.0, 4.0)
    query_out = jnp.clip(jax.random.normal(key_two, shape_query, jnp.float32), -4.0, 4.0)
    return (query_out, keys_out)


def draw_query(key, part):
    query_out, keys_out = paired_draw(key)
    return query_out.astype(jnp.bfloat16)


def draw_keys(key, part):
    query_out, keys_out = paired_draw(key)
    return keys_out.astype(jnp.bfloat16)


def shard_levels(key, extent, cuts, least, top_value):
    def one(axis_at, blocks):
        draws = jax.random.uniform(jax.random.fold_in(jax.random.fold_in(key, 6), axis_at), (blocks,), jnp.float32, least / len(cuts), top_value / len(cuts))
        return jnp.repeat(jnp.exp(draws), extent[axis_at] // blocks).reshape((-1,) + (1,) * (len(extent) - axis_at - 1))

    gain = one(*cuts[0])
    for cut in cuts[1:]:
        gain = gain * one(*cut)
    return gain


def profile(number_of, total, most, skew):
    weights = [(1 << 20) // math.isqrt(rank ** skew) + 1 for rank in range(2, number_of + 1)]
    rest, holding = total - most - (number_of - 1), [1] * (number_of - 1)
    while rest > 0:
        movable = [i for i in range(number_of - 1) if holding[i] < most]
        pool, left = sum([weights[i] for i in movable]), rest
        for i in movable:
            addition = min(most - holding[i], max(1, left * weights[i] // pool), rest)
            holding[i] = holding[i] + addition
            rest = rest - addition
    return np.array([most] + holding)


def uneven(own_key, number_of, total, most, skew):
    if number_of == 2:
        one = jax.random.randint(own_key, (), max(1, total - most), min(most, total - 1) + 1)
        return jnp.stack([one, total - one])
    sizes = jnp.asarray(profile(number_of, total, most, skew), jnp.int32)
    couples = (number_of - 1) // 2
    donor, receiver = sizes[1:1 + 2 * couples:2], sizes[2:2 + 2 * couples:2]
    margin = jnp.minimum(donor - 1, most - receiver)
    passed = jax.random.randint(jax.random.fold_in(own_key, 1), (couples,), 0, 1 << 20) % (margin + 1)
    sizes = sizes.at[1:1 + 2 * couples:2].set(donor - passed).at[2:2 + 2 * couples:2].set(receiver + passed)
    return sizes[jax.random.permutation(jax.random.fold_in(own_key, 2), number_of)]


def scatter_about(stream_key, shape, deviation, limit, cuts=(), held_as=jnp.bfloat16):
    drawn = jax.random.normal(stream_key, shape, jnp.float32) * deviation
    if len(cuts) > 0:
        drawn = shard_levels(stream_key, shape, cuts, -0.22, 0.18) * drawn
    return jnp.clip(drawn, min=-limit, max=limit).astype(held_as)


def setup_inputs(seed: int = 0) -> dict:
    arg_keys = jax.random.split(jax.random.key(seed), 6)
    return {
        "query": draw_query(jax.random.fold_in(arg_keys[5], 71), 0),
        "keys": draw_keys(jax.random.fold_in(arg_keys[5], 71), 0),
        "values": scatter_about(arg_keys[2], (SHARDS, 2, HALF, KV_HEADS * HEAD), 1.0, 6.0, ((0, 512),)),
        "grad_out": scatter_about(arg_keys[3], (SHARDS, 2, HALF, KV_HEADS * GROUP * HEAD), 1.0, 6.0, ((0, 512),)),
        "lengths": uneven(arg_keys[4], NDOC, LEN, DOC_MOST, 2).astype(jnp.int32),
    }


def to_order(blocks):
    early = blocks[:, 0]
    late = jnp.flip(blocks[:, 1], 0)
    return jnp.concatenate([early, late], 0).reshape(-1, blocks.shape[-1])

def from_order(flat, shards, half_rows):
    grouped = flat.reshape(2 * shards, half_rows, flat.shape[-1])
    return jnp.stack([grouped[:shards], jnp.flip(grouped[shards:], 0)], 1)

def reference(query, keys, values, grad_out, lengths):
    score_scale = 1.0 / math.sqrt(HEAD)
    window = DOC_MOST + HALF
    kv_width = KV_HEADS * HEAD
    flat_query = to_order(query).reshape(LEN, KV_HEADS, GROUP, HEAD)
    flat_keys = to_order(keys).reshape(LEN, KV_HEADS, HEAD)
    flat_values = to_order(values).reshape(LEN, KV_HEADS, HEAD)
    flat_grad = to_order(grad_out).reshape(LEN, KV_HEADS, GROUP, HEAD)
    doc_ends = jnp.cumsum(lengths).astype(jnp.int32)
    position = jnp.arange(LEN, dtype=jnp.int32)
    document = lax.optimization_barrier(jnp.sum((doc_ends[None, :] <= position[:, None]).astype(jnp.int32), axis=1)).astype(jnp.int32)
    pad_keys = jnp.concatenate([jnp.zeros((DOC_MOST, KV_HEADS, HEAD), flat_keys.dtype), flat_keys], 0)
    pad_values = jnp.concatenate([jnp.zeros((DOC_MOST, KV_HEADS, HEAD), flat_values.dtype), flat_values], 0)
    pad_doc = jnp.concatenate([jnp.full((DOC_MOST,), -1, jnp.int32), document], 0)

    def one_block(grad_pad, block):
        start = (block * HALF).astype(jnp.int32)
        block_query = lax.dynamic_slice_in_dim(flat_query, start, HALF, 0).astype(jnp.float32)
        block_grad = lax.dynamic_slice_in_dim(flat_grad, start, HALF, 0).astype(jnp.float32)
        key_win = lax.dynamic_slice_in_dim(pad_keys, start, window, 0).astype(jnp.float32)
        value_win = lax.dynamic_slice_in_dim(pad_values, start, window, 0).astype(jnp.float32)
        query_pos = start + jnp.arange(HALF, dtype=jnp.int32)
        query_doc = lax.dynamic_slice_in_dim(document, start, HALF, 0)
        key_pos = start - DOC_MOST + jnp.arange(window, dtype=jnp.int32)
        key_doc = lax.dynamic_slice_in_dim(pad_doc, start, window, 0)
        visible = (key_pos[None, :] <= query_pos[:, None]) & (key_doc[None, :] == query_doc[:, None])
        visible = visible[None, None]
        scores = jnp.einsum('qghd,kgd->ghqk', block_query, key_win) * score_scale
        masked = jnp.where(visible, scores, -1e+30)
        row_top = lax.optimization_barrier(jnp.max(masked, axis=3))
        summed = lax.optimization_barrier(jnp.sum(jnp.where(visible, jnp.exp(masked - row_top[..., None]), 0.0), axis=3))
        log_total = row_top + jnp.log(summed)
        probs = jnp.where(visible, jnp.exp(scores - log_total[..., None]), 0.0).astype(jnp.bfloat16)
        attn = jnp.einsum('ghqk,kgd->qghd', probs.astype(jnp.float32), value_win).astype(jnp.bfloat16)
        delta = jnp.transpose(lax.optimization_barrier(jnp.sum(block_grad * attn.astype(jnp.float32), axis=3)), (1, 2, 0))
        dprob = jnp.einsum('qghd,kgd->ghqk', block_grad, value_win)
        dscore = (probs.astype(jnp.float32) * (dprob - delta[..., None]) * score_scale).astype(jnp.bfloat16)
        query_grad = jnp.einsum('ghqk,kgd->qghd', dscore.astype(jnp.float32), key_win).astype(jnp.bfloat16)
        key_part = jnp.einsum('ghqk,qghd->kgd', dscore.astype(jnp.float32), block_query).reshape(window, kv_width)
        value_part = jnp.einsum('ghqk,qghd->kgd', probs.astype(jnp.float32), block_grad).reshape(window, kv_width)
        term = jnp.concatenate([key_part, value_part], 1)
        current = lax.dynamic_slice_in_dim(grad_pad, start, window, 0)
        grad_pad = lax.dynamic_update_slice_in_dim(grad_pad, current + term, start, 0)
        return (grad_pad, query_grad.reshape(HALF, KV_HEADS * GROUP * HEAD))
    blocks = jnp.arange(LEN // HALF, dtype=jnp.int32)
    grad_pad, query_blocks = lax.scan(one_block, jnp.zeros((LEN + DOC_MOST, 2 * kv_width), jnp.float32), blocks)
    grad_query_flat = query_blocks.reshape(LEN, KV_HEADS * GROUP * HEAD)
    grad_keys_flat = grad_pad[DOC_MOST:, :kv_width].astype(jnp.bfloat16)
    grad_values_flat = grad_pad[DOC_MOST:, kv_width:].astype(jnp.bfloat16)
    return (from_order(grad_query_flat, SHARDS, HALF), from_order(grad_keys_flat, SHARDS, HALF), from_order(grad_values_flat, SHARDS, HALF))
```

```python
import functools
import math

import jax
import jax.numpy as jnp
from jax import lax
from jax.experimental import pallas as pl
from jax.experimental.pallas import tpu as pltpu
from jax.sharding import PartitionSpec as P

HEAD = 128
REACH = 3
AXIS = ("dp", "ctx")


def shifted(value, steps):
    count = lax.axis_size(AXIS)
    pairs = [(s, s + steps) for s in range(count) if 0 <= s + steps < count]
    return lax.ppermute(value, AXIS, pairs)


def window_kernel(lo_ref, q_ref, do_ref, w0, w1, w2, w3, dq_ref, p0, p1, p2, p3, *, groups, group_size):
    half_rows = q_ref.shape[1]
    window = 4 * half_rows
    kv_width = groups * HEAD
    scale = 1.0 / math.sqrt(HEAD)
    lo = lo_ref[0]
    rows = lax.broadcasted_iota(jnp.int32, (half_rows, window), 0)
    cols = lax.broadcasted_iota(jnp.int32, (half_rows, window), 1)
    visible = (cols >= lo) & (cols <= rows + (window - half_rows))
    bias = jnp.where(visible, 0.0, -1e30).astype(jnp.float32)
    bias = jnp.concatenate([bias] * group_size, axis=0)
    wins = (w0, w1, w2, w3)
    outs = (p0, p1, p2, p3)
    for g in range(groups):
        base = g * group_size * HEAD
        qg = jnp.concatenate(
            [q_ref[0, :, base + h * HEAD:base + (h + 1) * HEAD] for h in range(group_size)], axis=0
        )
        dog = jnp.concatenate(
            [do_ref[0, :, base + h * HEAD:base + (h + 1) * HEAD] for h in range(group_size)], axis=0
        )
        kg = jnp.concatenate([w[0, :, g * HEAD:(g + 1) * HEAD] for w in wins], axis=0)
        vg = jnp.concatenate(
            [w[0, :, kv_width + g * HEAD:kv_width + (g + 1) * HEAD] for w in wins], axis=0
        )
        nt = (((1,), (1,)), ((), ()))
        tn = (((0,), (0,)), ((), ()))
        scores = lax.dot_general(qg, kg, nt, preferred_element_type=jnp.float32) * scale
        masked = scores + bias
        top = jnp.max(masked, axis=1, keepdims=True)
        expd = jnp.exp(masked - top)
        total = jnp.sum(expd, axis=1, keepdims=True)
        probs = (expd * (1.0 / total)).astype(jnp.bfloat16)
        attn = jnp.dot(probs, vg, preferred_element_type=jnp.float32).astype(jnp.bfloat16)
        delta = jnp.sum(dog.astype(jnp.float32) * attn.astype(jnp.float32), axis=1, keepdims=True)
        dprob = lax.dot_general(dog, vg, nt, preferred_element_type=jnp.float32)
        dscore = (probs.astype(jnp.float32) * (dprob - delta) * scale).astype(jnp.bfloat16)
        dq = jnp.dot(dscore, kg, preferred_element_type=jnp.float32).astype(jnp.bfloat16)
        for h in range(group_size):
            dq_ref[0, :, base + h * HEAD:base + (h + 1) * HEAD] = dq[h * half_rows:(h + 1) * half_rows]
        dk = lax.dot_general(dscore, qg, tn, preferred_element_type=jnp.float32)
        dv = lax.dot_general(probs, dog, tn, preferred_element_type=jnp.float32)
        for j in range(4):
            outs[j][0, :, g * HEAD:(g + 1) * HEAD] = dk[j * half_rows:(j + 1) * half_rows]
            outs[j][0, :, kv_width + g * HEAD:kv_width + (g + 1) * HEAD] = dv[
                j * half_rows:(j + 1) * half_rows
            ]


def window_grads(lo, q, do, wins):
    halves, half_rows, width = q.shape
    kv2 = wins[0].shape[2]
    groups = kv2 // (2 * HEAD)
    group_size = width // (groups * HEAD)
    kernel = functools.partial(window_kernel, groups=groups, group_size=group_size)
    q_spec = pl.BlockSpec((1, half_rows, width), lambda h: (h, 0, 0))
    w_spec = pl.BlockSpec((1, half_rows, kv2), lambda h: (h, 0, 0))
    lo_spec = pl.BlockSpec((1, half_rows, 1), lambda h: (h, 0, 0))
    flops = 6 * 2 * halves * groups * group_size * half_rows * 4 * half_rows * HEAD
    return pl.pallas_call(
        kernel,
        grid=(halves,),
        in_specs=[lo_spec, q_spec, q_spec] + [w_spec] * 4,
        out_specs=[q_spec] + [w_spec] * 4,
        out_shape=[jax.ShapeDtypeStruct(q.shape, jnp.bfloat16)]
        + [jax.ShapeDtypeStruct((halves, half_rows, kv2), jnp.float32)] * 4,
        cost_estimate=pl.CostEstimate(
            flops=flops,
            transcendentals=halves * groups * group_size * half_rows * 4 * half_rows,
            bytes_accessed=4 * q.size + 4 * 2 * wins[0].size + 4 * 4 * wins[0].size,
        ),
    )(lo, q, do, *wins)


def on_device(query, keys, values, grad_out, lengths):
    n = lax.axis_size(AXIS)
    me = lax.axis_index(AXIS)
    half_rows = query.shape[2]
    kv_width = keys.shape[3]
    q = query[0]
    do = grad_out[0]
    kv = jnp.concatenate([keys[0], values[0]], axis=2)
    early, late = kv[0], kv[1]
    at_top = me == n - 1
    below_top = me == n - 2

    e1 = shifted(early, 1)
    l1 = shifted(kv, -1)
    e2 = shifted(jnp.stack([early, e1]), 2)
    l2 = shifted(jnp.stack([late, jnp.where(at_top, early, l1[1])]), -2)
    late_slots = [
        jnp.where(at_top, e2[0], jnp.where(below_top, early, l2[1])),
        jnp.where(at_top, e1, jnp.where(below_top, l1[0], l2[0])),
        jnp.where(at_top, early, l1[1]),
        late,
    ]
    early_slots = [e2[1], e2[0], e1, early]
    wins = [jnp.stack([a, b]) for a, b in zip(early_slots, late_slots)]

    doc_ends = jnp.cumsum(lengths)
    block_ids = jnp.stack([me, 2 * n - 1 - me])
    query_pos = block_ids[:, None] * half_rows + jnp.arange(half_rows, dtype=jnp.int32)[None, :]
    ends = doc_ends[None, None, :]
    doc_start = jnp.max(jnp.where(ends <= query_pos[:, :, None], ends, 0), axis=2)
    lo = (doc_start - (block_ids[:, None] - REACH) * half_rows).astype(jnp.int32)[:, :, None]

    dq, p0, p1, p2, p3 = window_grads(lo, q, do, wins)

    zero = jnp.zeros_like(p0[0])
    p1e = p1[0] + jnp.where(at_top, p0[1], zero)
    p2e = p2[0] + jnp.where(at_top, p1[1], zero)
    a_e = shifted(jnp.stack([p1e, p0[0]]), -2)
    a_l = shifted(jnp.stack([p1[1], p0[1]]), 2)
    b_e = shifted(p2e + a_e[1], -1)
    b_l = shifted(jnp.stack([p2[1] + a_l[1], p1[1]]), 1)
    final_early = (
        p3[0]
        + a_e[0]
        + b_e
        + jnp.where(at_top, p2[1] + a_l[1] + b_l[1], zero)
        + jnp.where(below_top, p0[1], zero)
    )
    final_late = p3[1] + a_l[0] + b_l[0]
    final = jnp.stack([final_early, final_late])
    grad_keys = final[:, :, :kv_width].astype(jnp.bfloat16).reshape(keys.shape)
    grad_values = final[:, :, kv_width:].astype(jnp.bfloat16).reshape(values.shape)
    return (dq.reshape(query.shape), grad_keys, grad_values)


def solution(mesh):
    spec = P(AXIS, None, None, None)
    return jax.shard_map(
        on_device,
        mesh=mesh,
        in_specs=(spec, spec, spec, spec, P()),
        out_specs=(spec, spec, spec),
        check_vma=False,
    )
```

```python
import functools
import math

import jax
import jax.numpy as jnp
from jax import lax
from jax.experimental import pallas as pl
from jax.experimental.pallas import tpu as pltpu
from jax.sharding import PartitionSpec as P

HEAD = 128
REACH = 3
AXIS = ("dp", "ctx")


def shifted(value, steps):
    count = lax.axis_size(AXIS)
    pairs = [(s, s + steps) for s in range(count) if 0 <= s + steps < count]
    return lax.ppermute(value, AXIS, pairs)


def window_kernel(lo_ref, q_ref, do_ref, w0, w1, w2, w3, dq_ref, p0, p1, p2, p3, *, groups, group_size):
    half_rows = q_ref.shape[1]
    window = 4 * half_rows
    kv_width = groups * HEAD
    scale = 1.0 / math.sqrt(HEAD)
    lo = lo_ref[0]
    rows = lax.broadcasted_iota(jnp.int32, (half_rows, window), 0)
    cols = lax.broadcasted_iota(jnp.int32, (half_rows, window), 1)
    visible = (cols >= lo) & (cols <= rows + (window - half_rows))
    bias = jnp.where(visible, 0.0, -1e30).astype(jnp.float32)
    bias = jnp.concatenate([bias] * group_size, axis=0)
    wins = (w0, w1, w2, w3)
    outs = (p0, p1, p2, p3)
    for g in range(groups):
        base = g * group_size * HEAD
        qg = jnp.concatenate(
            [q_ref[0, :, base + h * HEAD:base + (h + 1) * HEAD] for h in range(group_size)], axis=0
        )
        dog = jnp.concatenate(
            [do_ref[0, :, base + h * HEAD:base + (h + 1) * HEAD] for h in range(group_size)], axis=0
        )
        kg = jnp.concatenate([w[0, :, g * HEAD:(g + 1) * HEAD] for w in wins], axis=0)
        vg = jnp.concatenate(
            [w[0, :, kv_width + g * HEAD:kv_width + (g + 1) * HEAD] for w in wins], axis=0
        )
        nt = (((1,), (1,)), ((), ()))
        tn = (((0,), (0,)), ((), ()))
        scores = lax.dot_general(qg, kg, nt, preferred_element_type=jnp.float32) * scale
        masked = scores + bias
        top = jnp.max(masked, axis=1, keepdims=True)
        expd = jnp.exp(masked - top)
        total = jnp.sum(expd, axis=1, keepdims=True)
        probs = (expd * (1.0 / total)).astype(jnp.bfloat16)
        attn = jnp.dot(probs, vg, preferred_element_type=jnp.float32).astype(jnp.bfloat16)
        delta = jnp.sum(dog.astype(jnp.float32) * attn.astype(jnp.float32), axis=1, keepdims=True)
        dprob = lax.dot_general(dog, vg, nt, preferred_element_type=jnp.float32)
        dscore = (probs.astype(jnp.float32) * (dprob - delta) * scale).astype(jnp.bfloat16)
        dq = jnp.dot(dscore, kg, preferred_element_type=jnp.float32).astype(jnp.bfloat16)
        for h in range(group_size):
            dq_ref[0, :, base + h * HEAD:base + (h + 1) * HEAD] = dq[h * half_rows:(h + 1) * half_rows]
        dk = lax.dot_general(dscore, qg, tn, preferred_element_type=jnp.float32)
        dv = lax.dot_general(probs, dog, tn, preferred_element_type=jnp.float32)
        for j in range(4):
            outs[j][0, :, g * HEAD:(g + 1) * HEAD] = dk[j * half_rows:(j + 1) * half_rows]
            outs[j][0, :, kv_width + g * HEAD:kv_width + (g + 1) * HEAD] = dv[
                j * half_rows:(j + 1) * half_rows
            ]


def window_grads(lo, q, do, wins):
    halves, half_rows, width = q.shape
    kv2 = wins[0].shape[2]
    groups = kv2 // (2 * HEAD)
    group_size = width // (groups * HEAD)
    kernel = functools.partial(window_kernel, groups=groups, group_size=group_size)
    q_spec = pl.BlockSpec((1, half_rows, width), lambda h: (h, 0, 0))
    w_spec = pl.BlockSpec((1, half_rows, kv2), lambda h: (h, 0, 0))
    lo_spec = pl.BlockSpec((1, half_rows, 1), lambda h: (h, 0, 0))
    flops = 6 * 2 * halves * groups * group_size * half_rows * 4 * half_rows * HEAD
    return pl.pallas_call(
        kernel,
        grid=(halves,),
        in_specs=[lo_spec, q_spec, q_spec] + [w_spec] * 4,
        out_specs=[q_spec] + [w_spec] * 4,
        out_shape=[jax.ShapeDtypeStruct(q.shape, jnp.bfloat16)]
        + [jax.ShapeDtypeStruct((halves, half_rows, kv2), jnp.float32)] * 4,
        cost_estimate=pl.CostEstimate(
            flops=flops,
            transcendentals=halves * groups * group_size * half_rows * 4 * half_rows,
            bytes_accessed=4 * q.size + 4 * 2 * wins[0].size + 4 * 4 * wins[0].size,
        ),
    )(lo, q, do, *wins)


def on_device(query, keys, values, grad_out, lengths):
    n = lax.axis_size(AXIS)
    me = lax.axis_index(AXIS)
    half_rows = query.shape[2]
    kv_width = keys.shape[3]
    q = query[0]
    do = grad_out[0]
    kv = jnp.concatenate([keys[0], values[0]], axis=2)
    early, late = kv[0], kv[1]
    at_top = me == n - 1
    below_top = me == n - 2

    e1 = shifted(early, 1)
    l1 = shifted(kv, -1)
    e2 = shifted(jnp.stack([early, e1]), 2)
    l2 = shifted(jnp.stack([late, jnp.where(at_top, early, l1[1])]), -2)
    late_slots = [
        jnp.where(at_top, e2[0], jnp.where(below_top, early, l2[1])),
        jnp.where(at_top, e1, jnp.where(below_top, l1[0], l2[0])),
        jnp.where(at_top, early, l1[1]),
        late,
    ]
    early_slots = [e2[1], e2[0], e1, early]
    wins = [jnp.stack([a, b]) for a, b in zip(early_slots, late_slots)]

    doc_ends = jnp.cumsum(lengths)
    block_ids = jnp.stack([me, 2 * n - 1 - me])
    query_pos = block_ids[:, None] * half_rows + jnp.arange(half_rows, dtype=jnp.int32)[None, :]
    ends = doc_ends[None, None, :]
    doc_start = jnp.max(jnp.where(ends <= query_pos[:, :, None], ends, 0), axis=2)
    lo = (doc_start - (block_ids[:, None] - REACH) * half_rows).astype(jnp.int32)[:, :, None]

    dq, p0, p1, p2, p3 = window_grads(lo, q, do, wins)

    zero = jnp.zeros_like(p0[0])
    link = jnp.bfloat16
    p1e = p1[0] + jnp.where(at_top, p0[1], zero)
    p2e = p2[0] + jnp.where(at_top, p1[1], zero)
    a_e = shifted(jnp.stack([p1e, p0[0]]).astype(link), -2).astype(jnp.float32)
    a_l = shifted(jnp.stack([p1[1], p0[1]]).astype(link), 2).astype(jnp.float32)
    b_e = shifted((p2e + a_e[1]).astype(link), -1).astype(jnp.float32)
    b_l = shifted(jnp.stack([p2[1] + a_l[1], p1[1]]).astype(link), 1).astype(jnp.float32)
    final_early = (
        p3[0]
        + a_e[0]
        + b_e
        + jnp.where(at_top, p2[1] + a_l[1] + b_l[1], zero)
        + jnp.where(below_top, p0[1], zero)
    )
    final_late = p3[1] + a_l[0] + b_l[0]
    final = jnp.stack([final_early, final_late])
    grad_keys = final[:, :, :kv_width].astype(jnp.bfloat16).reshape(keys.shape)
    grad_values = final[:, :, kv_width:].astype(jnp.bfloat16).reshape(values.shape)
    return (dq.reshape(query.shape), grad_keys, grad_values)


def solution(mesh):
    spec = P(AXIS, None, None, None)
    return jax.shard_map(
        on_device,
        mesh=mesh,
        in_specs=(spec, spec, spec, spec, P()),
        out_specs=(spec, spec, spec),
        check_vma=False,
    )
```

```python
import functools
import math

import jax
import jax.numpy as jnp
from jax import lax
from jax.experimental import pallas as pl
from jax.experimental.pallas import tpu as pltpu
from jax.sharding import PartitionSpec as P

HEAD = 128
REACH = 3
AXIS = ("dp", "ctx")


def shifted(value, steps):
    count = lax.axis_size(AXIS)
    pairs = [(s, s + steps) for s in range(count) if 0 <= s + steps < count]
    return lax.ppermute(value, AXIS, pairs)


def window_kernel(lo_ref, q_ref, do_ref, w0, w1, w2, w3, dq_ref, p0, p1, p2, p3, *, groups, group_size):
    half_rows = q_ref.shape[1]
    window = 4 * half_rows
    kv_width = groups * HEAD
    scale = 1.0 / math.sqrt(HEAD)
    lo = lo_ref[0]
    rows = lax.broadcasted_iota(jnp.int32, (half_rows, window), 0)
    cols = lax.broadcasted_iota(jnp.int32, (half_rows, window), 1)
    visible = (cols >= lo) & (cols <= rows + (window - half_rows))
    bias = jnp.where(visible, 0.0, -1e30).astype(jnp.float32)
    bias = jnp.concatenate([bias] * group_size, axis=0)
    wins = (w0, w1, w2, w3)
    outs = (p0, p1, p2, p3)
    for g in range(groups):
        base = g * group_size * HEAD
        qg = jnp.concatenate(
            [q_ref[0, :, base + h * HEAD:base + (h + 1) * HEAD] for h in range(group_size)], axis=0
        )
        dog = jnp.concatenate(
            [do_ref[0, :, base + h * HEAD:base + (h + 1) * HEAD] for h in range(group_size)], axis=0
        )
        kg = jnp.concatenate([w[0, :, g * HEAD:(g + 1) * HEAD] for w in wins], axis=0)
        vg = jnp.concatenate(
            [w[0, :, kv_width + g * HEAD:kv_width + (g + 1) * HEAD] for w in wins], axis=0
        )
        nt = (((1,), (1,)), ((), ()))
        tn = (((0,), (0,)), ((), ()))
        scores = lax.dot_general(qg, kg, nt, preferred_element_type=jnp.float32) * scale
        masked = scores + bias
        top = jnp.max(masked, axis=1, keepdims=True)
        expd = jnp.exp(masked - top)
        total = jnp.sum(expd, axis=1, keepdims=True)
        probs = (expd * (1.0 / total)).astype(jnp.bfloat16)
        attn = jnp.dot(probs, vg, preferred_element_type=jnp.float32).astype(jnp.bfloat16)
        delta = jnp.sum(dog.astype(jnp.float32) * attn.astype(jnp.float32), axis=1, keepdims=True)
        dprob = lax.dot_general(dog, vg, nt, preferred_element_type=jnp.float32)
        dscore = (probs.astype(jnp.float32) * (dprob - delta) * scale).astype(jnp.bfloat16)
        dq = jnp.dot(dscore, kg, preferred_element_type=jnp.float32).astype(jnp.bfloat16)
        for h in range(group_size):
            dq_ref[0, :, base + h * HEAD:base + (h + 1) * HEAD] = dq[h * half_rows:(h + 1) * half_rows]
        dk = lax.dot_general(dscore, qg, tn, preferred_element_type=jnp.float32)
        dv = lax.dot_general(probs, dog, tn, preferred_element_type=jnp.float32)
        for j in range(4):
            outs[j][0, :, g * HEAD:(g + 1) * HEAD] = dk[j * half_rows:(j + 1) * half_rows]
            outs[j][0, :, kv_width + g * HEAD:kv_width + (g + 1) * HEAD] = dv[
                j * half_rows:(j + 1) * half_rows
            ]


def window_grads(lo, q, do, wins):
    halves, half_rows, width = q.shape
    kv2 = wins[0].shape[2]
    groups = kv2 // (2 * HEAD)
    group_size = width // (groups * HEAD)
    kernel = functools.partial(window_kernel, groups=groups, group_size=group_size)
    q_spec = pl.BlockSpec((1, half_rows, width), lambda h: (h, 0, 0))
    w_spec = pl.BlockSpec((1, half_rows, kv2), lambda h: (h, 0, 0))
    lo_spec = pl.BlockSpec((1, half_rows, 1), lambda h: (h, 0, 0))
    flops = 6 * 2 * halves * groups * group_size * half_rows * 4 * half_rows * HEAD
    return pl.pallas_call(
        kernel,
        grid=(halves,),
        in_specs=[lo_spec, q_spec, q_spec] + [w_spec] * 4,
        out_specs=[q_spec] + [w_spec] * 4,
        out_shape=[jax.ShapeDtypeStruct(q.shape, jnp.bfloat16)]
        + [jax.ShapeDtypeStruct((halves, half_rows, kv2), jnp.float32)] * 4,
        cost_estimate=pl.CostEstimate(
            flops=flops,
            transcendentals=halves * groups * group_size * half_rows * 4 * half_rows,
            bytes_accessed=4 * q.size + 4 * 2 * wins[0].size + 4 * 4 * wins[0].size,
        ),
    )(lo, q, do, *wins)


def on_device(query, keys, values, grad_out, lengths):
    n = lax.axis_size(AXIS)
    me = lax.axis_index(AXIS)
    half_rows = query.shape[2]
    kv_width = keys.shape[3]
    q = query[0]
    do = grad_out[0]
    kv = jnp.concatenate([keys[0], values[0]], axis=2)
    early, late = kv[0], kv[1]
    at_top = me == n - 1
    below_top = me == n - 2

    e1, e2, e3 = (shifted(early, k) for k in (1, 2, 3))
    l1, l2 = (shifted(kv, -k) for k in (1, 2))
    l3 = shifted(late, -3)
    late_slots = [
        jnp.where(at_top, e2, jnp.where(below_top, early, jnp.where(me == n - 3, l2[0], l3))),
        jnp.where(at_top, e1, jnp.where(below_top, l1[0], l2[1])),
        jnp.where(at_top, early, l1[1]),
        late,
    ]
    early_slots = [e3, e2, e1, early]
    wins = [jnp.stack([a, b]) for a, b in zip(early_slots, late_slots)]

    doc_ends = jnp.cumsum(lengths)
    block_ids = jnp.stack([me, 2 * n - 1 - me])
    query_pos = block_ids[:, None] * half_rows + jnp.arange(half_rows, dtype=jnp.int32)[None, :]
    ends = doc_ends[None, None, :]
    doc_start = jnp.max(jnp.where(ends <= query_pos[:, :, None], ends, 0), axis=2)
    lo = (doc_start - (block_ids[:, None] - REACH) * half_rows).astype(jnp.int32)[:, :, None]

    dq, p0, p1, p2, p3 = window_grads(lo, q, do, wins)

    zero = jnp.zeros_like(p0[0])
    link = jnp.bfloat16
    p1e = p1[0] + jnp.where(at_top, p0[1], zero)
    p2e = p2[0] + jnp.where(at_top, p1[1], zero)
    r_e1 = shifted(p2e.astype(link), -1).astype(jnp.float32)
    r_e2 = shifted(p1e.astype(link), -2).astype(jnp.float32)
    r_e3 = shifted(p0[0].astype(link), -3).astype(jnp.float32)
    r_l1 = shifted(jnp.stack([p2[1], p1[1]]).astype(link), 1).astype(jnp.float32)
    r_l2 = shifted(jnp.stack([p1[1], p0[1]]).astype(link), 2).astype(jnp.float32)
    r_l3 = shifted(p0[1].astype(link), 3).astype(jnp.float32)
    final_early = (
        p3[0]
        + r_e1
        + r_e2
        + r_e3
        + jnp.where(at_top, p2[1] + r_l1[1] + r_l2[1], zero)
        + jnp.where(below_top, p0[1], zero)
    )
    final_late = p3[1] + r_l1[0] + r_l2[0] + r_l3
    final = jnp.stack([final_early, final_late])
    grad_keys = final[:, :, :kv_width].astype(jnp.bfloat16).reshape(keys.shape)
    grad_values = final[:, :, kv_width:].astype(jnp.bfloat16).reshape(values.shape)
    return (dq.reshape(query.shape), grad_keys, grad_values)


def solution(mesh):
    spec = P(AXIS, None, None, None)
    return jax.shard_map(
        on_device,
        mesh=mesh,
        in_specs=(spec, spec, spec, spec, P()),
        out_specs=(spec, spec, spec),
        check_vma=False,
    )
```

```python
import functools
import math

import jax
import jax.numpy as jnp
from jax import lax
from jax.experimental import pallas as pl
from jax.experimental.pallas import tpu as pltpu
from jax.sharding import PartitionSpec as P

HEAD = 128
REACH = 3
AXIS = ("dp", "ctx")


def shifted(value, steps):
    count = lax.axis_size(AXIS)
    pairs = [(s, s + steps) for s in range(count) if 0 <= s + steps < count]
    return lax.ppermute(value, AXIS, pairs)


def window_kernel(lo_ref, q_ref, do_ref, w0, w1, w2, w3, dq_ref, p0, p1, p2, p3, *, groups, group_size):
    half_rows = q_ref.shape[1]
    window = 4 * half_rows
    kv_width = groups * HEAD
    scale = 1.0 / math.sqrt(HEAD)
    lo = lo_ref[0]
    rows = lax.broadcasted_iota(jnp.int32, (half_rows, window), 0)
    cols = lax.broadcasted_iota(jnp.int32, (half_rows, window), 1)
    visible = (cols >= lo) & (cols <= rows + (window - half_rows))
    bias = jnp.where(visible, 0.0, -1e30).astype(jnp.float32)
    bias = jnp.concatenate([bias] * group_size, axis=0)
    wins = (w0, w1, w2, w3)
    outs = (p0, p1, p2, p3)
    for g in range(groups):
        base = g * group_size * HEAD
        qg = jnp.concatenate(
            [q_ref[0, :, base + h * HEAD:base + (h + 1) * HEAD] for h in range(group_size)], axis=0
        )
        dog = jnp.concatenate(
            [do_ref[0, :, base + h * HEAD:base + (h + 1) * HEAD] for h in range(group_size)], axis=0
        )
        kg = jnp.concatenate([w[0, :, g * HEAD:(g + 1) * HEAD] for w in wins], axis=0)
        vg = jnp.concatenate(
            [w[0, :, kv_width + g * HEAD:kv_width + (g + 1) * HEAD] for w in wins], axis=0
        )
        nt = (((1,), (1,)), ((), ()))
        tn = (((0,), (0,)), ((), ()))
        scores = lax.dot_general(qg, kg, nt, preferred_element_type=jnp.float32) * scale
        masked = scores + bias
        top = jnp.max(masked, axis=1, keepdims=True)
        expd = jnp.exp(masked - top)
        total = jnp.sum(expd, axis=1, keepdims=True)
        probs = (expd * (1.0 / total)).astype(jnp.bfloat16)
        attn = jnp.dot(probs, vg, preferred_element_type=jnp.float32).astype(jnp.bfloat16)
        delta = jnp.sum(dog.astype(jnp.float32) * attn.astype(jnp.float32), axis=1, keepdims=True)
        dprob = lax.dot_general(dog, vg, nt, preferred_element_type=jnp.float32)
        dscore = (probs.astype(jnp.float32) * (dprob - delta) * scale).astype(jnp.bfloat16)
        dq = jnp.dot(dscore, kg, preferred_element_type=jnp.float32).astype(jnp.bfloat16)
        for h in range(group_size):
            dq_ref[0, :, base + h * HEAD:base + (h + 1) * HEAD] = dq[h * half_rows:(h + 1) * half_rows]
        dk = lax.dot_general(dscore, qg, tn, preferred_element_type=jnp.float32)
        dv = lax.dot_general(probs, dog, tn, preferred_element_type=jnp.float32)
        for j in range(4):
            outs[j][0, :, g * HEAD:(g + 1) * HEAD] = dk[j * half_rows:(j + 1) * half_rows]
            outs[j][0, :, kv_width + g * HEAD:kv_width + (g + 1) * HEAD] = dv[
                j * half_rows:(j + 1) * half_rows
            ]


def window_grads(lo, q, do, wins):
    halves, half_rows, width = q.shape
    kv2 = wins[0].shape[2]
    groups = kv2 // (2 * HEAD)
    group_size = width // (groups * HEAD)
    kernel = functools.partial(window_kernel, groups=groups, group_size=group_size)
    q_spec = pl.BlockSpec((1, half_rows, width), lambda h: (h, 0, 0))
    w_spec = pl.BlockSpec((1, half_rows, kv2), lambda h: (h, 0, 0))
    lo_spec = pl.BlockSpec((1, half_rows, 1), lambda h: (h, 0, 0))
    flops = 6 * 2 * halves * groups * group_size * half_rows * 4 * half_rows * HEAD
    return pl.pallas_call(
        kernel,
        grid=(halves,),
        in_specs=[lo_spec, q_spec, q_spec] + [w_spec] * 4,
        out_specs=[q_spec] + [w_spec] * 4,
        out_shape=[jax.ShapeDtypeStruct(q.shape, jnp.bfloat16)]
        + [jax.ShapeDtypeStruct((halves, half_rows, kv2), jnp.float32)] * 4,
        cost_estimate=pl.CostEstimate(
            flops=flops,
            transcendentals=halves * groups * group_size * half_rows * 4 * half_rows,
            bytes_accessed=4 * q.size + 4 * 2 * wins[0].size + 4 * 4 * wins[0].size,
        ),
    )(lo, q, do, *wins)


def on_device(query, keys, values, grad_out, lengths):
    n = lax.axis_size(AXIS)
    me = lax.axis_index(AXIS)
    half_rows = query.shape[2]
    kv_width = keys.shape[3]
    q = query[0]
    do = grad_out[0]
    kv = jnp.concatenate([keys[0], values[0]], axis=2)
    early, late = kv[0], kv[1]
    at_top = me == n - 1
    below_top = me == n - 2

    e1 = shifted(early, 1)
    l1 = shifted(late, -1)
    turn = lax.ppermute(early, AXIS, [(n - 1, n - 2)])
    e2 = shifted(jnp.stack([early, e1]), 2)
    l2 = shifted(jnp.stack([late, jnp.where(at_top, early, l1)]), -2)
    late_slots = [
        jnp.where(at_top, e2[0], jnp.where(below_top, early, l2[1])),
        jnp.where(at_top, e1, jnp.where(below_top, turn, l2[0])),
        jnp.where(at_top, early, l1),
        late,
    ]
    early_slots = [e2[1], e2[0], e1, early]
    wins = [jnp.stack([a, b]) for a, b in zip(early_slots, late_slots)]

    doc_ends = jnp.cumsum(lengths)
    block_ids = jnp.stack([me, 2 * n - 1 - me])
    query_pos = block_ids[:, None] * half_rows + jnp.arange(half_rows, dtype=jnp.int32)[None, :]
    ends = doc_ends[None, None, :]
    doc_start = jnp.max(jnp.where(ends <= query_pos[:, :, None], ends, 0), axis=2)
    lo = (doc_start - (block_ids[:, None] - REACH) * half_rows).astype(jnp.int32)[:, :, None]

    dq, p0, p1, p2, p3 = window_grads(lo, q, do, wins)

    zero = jnp.zeros_like(p0[0])
    link = jnp.bfloat16
    p1e = p1[0] + jnp.where(at_top, p0[1], zero)
    p2e = p2[0] + jnp.where(at_top, p1[1], zero)
    a_e = shifted(jnp.stack([p1e, p0[0]]).astype(link), -2).astype(jnp.float32)
    a_l = shifted(jnp.stack([p1[1], p0[1]]).astype(link), 2).astype(jnp.float32)
    b_e = shifted((p2e + a_e[1]).astype(link), -1).astype(jnp.float32)
    b_l = shifted((p2[1] + a_l[1]).astype(link), 1).astype(jnp.float32)
    back = lax.ppermute(p1[1].astype(link), AXIS, [(n - 2, n - 1)]).astype(jnp.float32)
    final_early = (
        p3[0]
        + a_e[0]
        + b_e
        + jnp.where(at_top, p2[1] + a_l[1] + back, zero)
        + jnp.where(below_top, p0[1], zero)
    )
    final_late = p3[1] + a_l[0] + b_l
    final = jnp.stack([final_early, final_late])
    grad_keys = final[:, :, :kv_width].astype(jnp.bfloat16).reshape(keys.shape)
    grad_values = final[:, :, kv_width:].astype(jnp.bfloat16).reshape(values.shape)
    return (dq.reshape(query.shape), grad_keys, grad_values)


def solution(mesh):
    spec = P(AXIS, None, None, None)
    return jax.shard_map(
        on_device,
        mesh=mesh,
        in_specs=(spec, spec, spec, spec, P()),
        out_specs=(spec, spec, spec),
        check_vma=False,
    )
```

```python
import functools
import math

import jax
import jax.numpy as jnp
from jax import lax
from jax.experimental import pallas as pl
from jax.experimental.pallas import tpu as pltpu
from jax.sharding import PartitionSpec as P

HEAD = 128
REACH = 3
AXIS = ("dp", "ctx")


def shifted(value, steps):
    count = lax.axis_size(AXIS)
    pairs = [(s, s + steps) for s in range(count) if 0 <= s + steps < count]
    return lax.ppermute(value, AXIS, pairs)


def window_half(half, slot, lo_ref, q_ref, do_ref, groups, group_size, emit):
    half_rows = q_ref.shape[1]
    window = 4 * half_rows
    kv_width = groups * HEAD
    scale = 1.0 / math.sqrt(HEAD)
    lo = lo_ref[0]
    rows = lax.broadcasted_iota(jnp.int32, (half_rows, window), 0)
    cols = lax.broadcasted_iota(jnp.int32, (half_rows, window), 1)
    visible = (cols >= lo) & (cols <= rows + (window - half_rows))
    bias = jnp.where(visible, 0.0, -1e30).astype(jnp.float32)
    bias = jnp.concatenate([bias] * group_size, axis=0)
    nt = (((1,), (1,)), ((), ()))
    tn = (((0,), (0,)), ((), ()))
    for g in range(groups):
        base = g * group_size * HEAD
        qg = jnp.concatenate(
            [q_ref[0, :, base + h * HEAD:base + (h + 1) * HEAD] for h in range(group_size)], axis=0
        )
        dog = jnp.concatenate(
            [do_ref[0, :, base + h * HEAD:base + (h + 1) * HEAD] for h in range(group_size)], axis=0
        )
        kg = jnp.concatenate([slot(j, g * HEAD) for j in range(4)], axis=0)
        vg = jnp.concatenate([slot(j, kv_width + g * HEAD) for j in range(4)], axis=0)
        scores = lax.dot_general(qg, kg, nt, preferred_element_type=jnp.float32) * scale
        masked = scores + bias
        top = jnp.max(masked, axis=1, keepdims=True)
        expd = jnp.exp(masked - top)
        total = jnp.sum(expd, axis=1, keepdims=True)
        probs = (expd * (1.0 / total)).astype(jnp.bfloat16)
        attn = jnp.dot(probs, vg, preferred_element_type=jnp.float32).astype(jnp.bfloat16)
        delta = jnp.sum(dog.astype(jnp.float32) * attn.astype(jnp.float32), axis=1, keepdims=True)
        dprob = lax.dot_general(dog, vg, nt, preferred_element_type=jnp.float32)
        dscore = (probs.astype(jnp.float32) * (dprob - delta) * scale).astype(jnp.bfloat16)
        dq = jnp.dot(dscore, kg, preferred_element_type=jnp.float32).astype(jnp.bfloat16)
        for h in range(group_size):
            emit("dq", h, base + h * HEAD, dq[h * half_rows:(h + 1) * half_rows])
        dk = lax.dot_general(dscore, qg, tn, preferred_element_type=jnp.float32)
        dv = lax.dot_general(probs, dog, tn, preferred_element_type=jnp.float32)
        for j in range(4):
            emit("part", j, g * HEAD, dk[j * half_rows:(j + 1) * half_rows])
            emit("part", j, kv_width + g * HEAD, dv[j * half_rows:(j + 1) * half_rows])


def window_kernel(
    flags, lo_ref, q_ref, do_ref, kv, e1, e2, l1, l2, turn,
    dq_ref, a_e, a_l, p2_ref, p3_ref, kept, *, groups, group_size
):
    step = pl.program_id(0)
    at_top = flags[0] != 0
    below_top = flags[1] != 0

    def tile(ref, lanes, *lead):
        return ref[lead + (slice(None), pl.ds(lanes, HEAD))]

    def store_dq(h, lanes, value):
        dq_ref[0, :, pl.ds(lanes, HEAD)] = value

    def late_slot(j, lanes):
        if j == 0:
            regular = jnp.where(below_top, tile(kv, lanes, 0), tile(l2, lanes, 1))
            return jnp.where(at_top, tile(e2, lanes, 0), regular)
        if j == 1:
            regular = jnp.where(below_top, tile(turn, lanes), tile(l2, lanes, 0))
            return jnp.where(at_top, tile(e1, lanes), regular)
        if j == 2:
            return jnp.where(at_top, tile(kv, lanes, 0), tile(l1, lanes))
        return tile(kv, lanes, 1)

    def early_slot(j, lanes):
        return (
            tile(e2, lanes, 1), tile(e2, lanes, 0), tile(e1, lanes), tile(kv, lanes, 0)
        )[j]

    def late_emit(kind, j, lanes, value):
        if kind == "dq":
            store_dq(j, lanes, value)
            return
        cols = pl.ds(lanes, HEAD)
        if j < 3:
            kept[j, :, cols] = value
        if j == 0:
            a_l[1, :, cols] = value.astype(a_l.dtype)
        elif j == 1:
            a_l[0, :, cols] = value.astype(a_l.dtype)
        elif j == 2:
            p2_ref[0, :, cols] = value.astype(p2_ref.dtype)
        else:
            p3_ref[0, :, cols] = value

    def early_emit(kind, j, lanes, value):
        if kind == "dq":
            store_dq(j, lanes, value)
            return
        cols = pl.ds(lanes, HEAD)
        zero = jnp.zeros_like(value)
        if j == 0:
            a_e[1, :, cols] = value.astype(a_e.dtype)
        elif j == 1:
            merged = value + jnp.where(at_top, kept[0, :, cols], zero)
            a_e[0, :, cols] = merged.astype(a_e.dtype)
        elif j == 2:
            merged = value + jnp.where(at_top, kept[1, :, cols], zero)
            p2_ref[0, :, cols] = merged.astype(p2_ref.dtype)
        else:
            merged = (
                value
                + jnp.where(at_top, kept[2, :, cols], zero)
                + jnp.where(below_top, kept[0, :, cols], zero)
            )
            p3_ref[0, :, cols] = merged

    @pl.when(step == 0)
    def _():
        window_half(1, late_slot, lo_ref, q_ref, do_ref, groups, group_size, late_emit)

    @pl.when(step == 1)
    def _():
        window_half(0, early_slot, lo_ref, q_ref, do_ref, groups, group_size, early_emit)


def window_grads(flags, lo, q, do, kv, e1, e2, l1, l2, turn):
    halves, half_rows, width = q.shape
    kv2 = kv.shape[2]
    groups = kv2 // (2 * HEAD)
    group_size = width // (groups * HEAD)
    kernel = functools.partial(window_kernel, groups=groups, group_size=group_size)
    q_spec = pl.BlockSpec((1, half_rows, width), lambda s: (1 - s, 0, 0))
    lo_spec = pl.BlockSpec((1, half_rows, 1), lambda s: (1 - s, 0, 0))
    part_spec = pl.BlockSpec((1, half_rows, kv2), lambda s: (1 - s, 0, 0))
    pair_spec = pl.BlockSpec((2, half_rows, kv2), lambda s: (0, 0, 0))
    one_spec = pl.BlockSpec((half_rows, kv2), lambda s: (0, 0))
    flops = 6 * 2 * halves * groups * group_size * half_rows * 4 * half_rows * HEAD
    pair = jax.ShapeDtypeStruct((2, half_rows, kv2), jnp.bfloat16)
    return pl.pallas_call(
        kernel,
        grid=(halves,),
        in_specs=[
            pl.BlockSpec(memory_space=pltpu.SMEM),
            lo_spec,
            q_spec,
            q_spec,
            pair_spec,
            one_spec,
            pair_spec,
            one_spec,
            pair_spec,
            one_spec,
        ],
        out_specs=[q_spec, pair_spec, pair_spec, part_spec, part_spec],
        out_shape=[
            jax.ShapeDtypeStruct(q.shape, jnp.bfloat16),
            pair,
            pair,
            jax.ShapeDtypeStruct((halves, half_rows, kv2), jnp.bfloat16),
            jax.ShapeDtypeStruct((halves, half_rows, kv2), jnp.float32),
        ],
        scratch_shapes=[pltpu.VMEM((3, half_rows, kv2), jnp.float32)],
        cost_estimate=pl.CostEstimate(
            flops=flops,
            transcendentals=halves * groups * group_size * half_rows * 4 * half_rows,
            bytes_accessed=4 * q.size + 10 * kv.size,
        ),
    )(flags, lo, q, do, kv, e1, e2, l1, l2, turn)


def on_device(query, keys, values, grad_out, lengths):
    n = lax.axis_size(AXIS)
    me = lax.axis_index(AXIS)
    half_rows = query.shape[2]
    kv_width = keys.shape[3]
    q = query[0]
    do = grad_out[0]
    kv = jnp.concatenate([keys[0], values[0]], axis=2)
    early, late = kv[0], kv[1]
    at_top = me == n - 1
    below_top = me == n - 2

    e1 = shifted(early, 1)
    l1 = shifted(late, -1)
    turn = lax.ppermute(early, AXIS, [(n - 1, n - 2)])
    e2 = shifted(jnp.stack([early, e1]), 2)
    l2 = shifted(jnp.stack([late, jnp.where(at_top, early, l1)]), -2)

    doc_ends = jnp.cumsum(lengths)
    block_ids = jnp.stack([me, 2 * n - 1 - me])
    query_pos = block_ids[:, None] * half_rows + jnp.arange(half_rows, dtype=jnp.int32)[None, :]
    ends = doc_ends[None, None, :]
    doc_start = jnp.max(jnp.where(ends <= query_pos[:, :, None], ends, 0), axis=2)
    lo = (doc_start - (block_ids[:, None] - REACH) * half_rows).astype(jnp.int32)[:, :, None]
    flags = jnp.stack([at_top, below_top]).astype(jnp.int32)

    dq, a_e, a_l, p2, p3 = window_grads(flags, lo, q, do, kv, e1, e2, l1, l2, turn)

    zero = jnp.zeros_like(p3[0])
    link = jnp.bfloat16
    a_e = shifted(a_e, -2).astype(jnp.float32)
    back = lax.ppermute(a_l[0], AXIS, [(n - 2, n - 1)]).astype(jnp.float32)
    a_l = shifted(a_l, 2).astype(jnp.float32)
    b_e = shifted((p2[0].astype(jnp.float32) + a_e[1]).astype(link), -1).astype(jnp.float32)
    b_l = shifted((p2[1].astype(jnp.float32) + a_l[1]).astype(link), 1).astype(jnp.float32)
    final_early = p3[0] + a_e[0] + b_e + jnp.where(at_top, a_l[1] + back, zero)
    final_late = p3[1] + a_l[0] + b_l
    final = jnp.stack([final_early, final_late])
    grad_keys = final[:, :, :kv_width].astype(jnp.bfloat16).reshape(keys.shape)
    grad_values = final[:, :, kv_width:].astype(jnp.bfloat16).reshape(values.shape)
    return (dq.reshape(query.shape), grad_keys, grad_values)


def solution(mesh):
    spec = P(AXIS, None, None, None)
    return jax.shard_map(
        on_device,
        mesh=mesh,
        in_specs=(spec, spec, spec, spec, P()),
        out_specs=(spec, spec, spec),
        check_vma=False,
    )
```

```python
import functools
import math

import jax
import jax.numpy as jnp
from jax import lax
from jax.experimental import pallas as pl
from jax.experimental.pallas import tpu as pltpu
from jax.sharding import PartitionSpec as P

HEAD = 128
REACH = 3
AXIS = ("dp", "ctx")


def shifted(value, steps):
    count = lax.axis_size(AXIS)
    pairs = [(s, s + steps) for s in range(count) if 0 <= s + steps < count]
    return lax.ppermute(value, AXIS, pairs)


def window_half(half, slot, lo_ref, q_ref, do_ref, groups, group_size, emit):
    half_rows = q_ref.shape[1]
    window = 4 * half_rows
    kv_width = groups * HEAD
    scale = 1.0 / math.sqrt(HEAD)
    lo = lo_ref[0]
    rows = lax.broadcasted_iota(jnp.int32, (half_rows, window), 0)
    cols = lax.broadcasted_iota(jnp.int32, (half_rows, window), 1)
    visible = (cols >= lo) & (cols <= rows + (window - half_rows))
    bias = jnp.where(visible, 0.0, -1e30).astype(jnp.float32)
    bias = jnp.concatenate([bias] * group_size, axis=0)
    nt = (((1,), (1,)), ((), ()))
    tn = (((0,), (0,)), ((), ()))
    for g in range(groups):
        base = g * group_size * HEAD
        qg = jnp.concatenate(
            [q_ref[0, :, base + h * HEAD:base + (h + 1) * HEAD] for h in range(group_size)], axis=0
        )
        dog = jnp.concatenate(
            [do_ref[0, :, base + h * HEAD:base + (h + 1) * HEAD] for h in range(group_size)], axis=0
        )
        kg = jnp.concatenate([slot(j, g * HEAD) for j in range(4)], axis=0)
        vg = jnp.concatenate([slot(j, kv_width + g * HEAD) for j in range(4)], axis=0)
        scores = lax.dot_general(qg, kg, nt, preferred_element_type=jnp.float32) * scale
        masked = scores + bias
        top = jnp.max(masked, axis=1, keepdims=True)
        expd = jnp.exp(masked - top)
        total = jnp.sum(expd, axis=1, keepdims=True)
        probs = (expd * (1.0 / total)).astype(jnp.bfloat16)
        attn = jnp.dot(probs, vg, preferred_element_type=jnp.float32).astype(jnp.bfloat16)
        delta = jnp.sum(dog.astype(jnp.float32) * attn.astype(jnp.float32), axis=1, keepdims=True)
        dprob = lax.dot_general(dog, vg, nt, preferred_element_type=jnp.float32)
        dscore = (probs.astype(jnp.float32) * (dprob - delta) * scale).astype(jnp.bfloat16)
        dq = jnp.dot(dscore, kg, preferred_element_type=jnp.float32).astype(jnp.bfloat16)
        for h in range(group_size):
            emit("dq", h, base + h * HEAD, dq[h * half_rows:(h + 1) * half_rows])
        dk = lax.dot_general(dscore, qg, tn, preferred_element_type=jnp.float32)
        dv = lax.dot_general(probs, dog, tn, preferred_element_type=jnp.float32)
        for j in range(4):
            emit("part", j, g * HEAD, dk[j * half_rows:(j + 1) * half_rows])
            emit("part", j, kv_width + g * HEAD, dv[j * half_rows:(j + 1) * half_rows])


def late_kernel(
    flags, lo_ref, q_ref, do_ref, kv, l1, l2, turn2, turn3,
    dq_ref, a_l, p2_ref, p3_ref, kept, *, groups, group_size
):
    at_top = flags[0] != 0
    below_top = flags[1] != 0

    def slot(j, lanes):
        cols = pl.ds(lanes, HEAD)
        if j == 0:
            regular = jnp.where(below_top, kv[0, :, cols], l2[1, :, cols])
            return jnp.where(at_top, turn3[:, cols], regular)
        if j == 1:
            return jnp.where(at_top | below_top, turn2[:, cols], l2[0, :, cols])
        if j == 2:
            return jnp.where(at_top, kv[0, :, cols], l1[:, cols])
        return kv[1, :, cols]

    def emit(kind, j, lanes, value):
        cols = pl.ds(lanes, HEAD)
        if kind == "dq":
            dq_ref[0, :, cols] = value
            return
        if j < 3:
            kept[j, :, cols] = value
        if j == 0:
            a_l[1, :, cols] = value.astype(a_l.dtype)
        elif j == 1:
            a_l[0, :, cols] = value.astype(a_l.dtype)
        elif j == 2:
            p2_ref[0, :, cols] = value.astype(p2_ref.dtype)
        else:
            p3_ref[0, :, cols] = value

    window_half(1, slot, lo_ref, q_ref, do_ref, groups, group_size, emit)


def early_kernel(
    flags, lo_ref, q_ref, do_ref, kv, e1, e2, kept, dq_in, p2_in, p3_in,
    dq_ref, a_e, p2_ref, p3_ref, *, groups, group_size
):
    del dq_in, p2_in, p3_in
    at_top = flags[0] != 0
    below_top = flags[1] != 0

    def slot(j, lanes):
        cols = pl.ds(lanes, HEAD)
        return (e2[1, :, cols], e2[0, :, cols], e1[:, cols], kv[0, :, cols])[j]

    def emit(kind, j, lanes, value):
        cols = pl.ds(lanes, HEAD)
        if kind == "dq":
            dq_ref[0, :, cols] = value
            return
        zero = jnp.zeros_like(value)
        if j == 0:
            a_e[1, :, cols] = value.astype(a_e.dtype)
        elif j == 1:
            merged = value + jnp.where(at_top, kept[0, :, cols], zero)
            a_e[0, :, cols] = merged.astype(a_e.dtype)
        elif j == 2:
            merged = value + jnp.where(at_top, kept[1, :, cols], zero)
            p2_ref[0, :, cols] = merged.astype(p2_ref.dtype)
        else:
            merged = (
                value
                + jnp.where(at_top, kept[2, :, cols], zero)
                + jnp.where(below_top, kept[0, :, cols], zero)
            )
            p3_ref[0, :, cols] = merged

    window_half(0, slot, lo_ref, q_ref, do_ref, groups, group_size, emit)


def window_grads(flags, lo, q, do, kv, e1, e2, l1, l2, turn2, turn3):
    halves, half_rows, width = q.shape
    kv2 = kv.shape[2]
    groups = kv2 // (2 * HEAD)
    group_size = width // (groups * HEAD)
    flops = 6 * 2 * groups * group_size * half_rows * 4 * half_rows * HEAD
    cost = pl.CostEstimate(
        flops=flops,
        transcendentals=groups * group_size * half_rows * 4 * half_rows,
        bytes_accessed=2 * q.size + 6 * kv.size,
    )

    def half_specs(half):
        q_spec = pl.BlockSpec((1, half_rows, width), lambda s: (half, 0, 0))
        lo_spec = pl.BlockSpec((1, half_rows, 1), lambda s: (half, 0, 0))
        part_spec = pl.BlockSpec((1, half_rows, kv2), lambda s: (half, 0, 0))
        return q_spec, lo_spec, part_spec

    pair_spec = pl.BlockSpec((2, half_rows, kv2), lambda s: (0, 0, 0))
    one_spec = pl.BlockSpec((half_rows, kv2), lambda s: (0, 0))
    kept_spec = pl.BlockSpec((3, half_rows, kv2), lambda s: (0, 0, 0))
    smem = pl.BlockSpec(memory_space=pltpu.SMEM)
    anywhere = pl.BlockSpec(memory_space=pl.ANY)
    pair = jax.ShapeDtypeStruct((2, half_rows, kv2), jnp.bfloat16)
    dq_shape = jax.ShapeDtypeStruct(q.shape, jnp.bfloat16)
    p2_shape = jax.ShapeDtypeStruct((halves, half_rows, kv2), jnp.bfloat16)
    p3_shape = jax.ShapeDtypeStruct((halves, half_rows, kv2), jnp.float32)

    q_spec, lo_spec, part_spec = half_specs(1)
    dq, a_l, p2, p3, kept = pl.pallas_call(
        functools.partial(late_kernel, groups=groups, group_size=group_size),
        grid=(1,),
        in_specs=[smem, lo_spec, q_spec, q_spec, pair_spec, one_spec, pair_spec, one_spec, one_spec],
        out_specs=[q_spec, pair_spec, part_spec, part_spec, kept_spec],
        out_shape=[
            dq_shape, pair, p2_shape, p3_shape,
            jax.ShapeDtypeStruct((3, half_rows, kv2), jnp.float32),
        ],
        cost_estimate=cost,
    )(flags, lo, q, do, kv, l1, l2, turn2, turn3)

    q_spec, lo_spec, part_spec = half_specs(0)
    dq, a_e, p2, p3 = pl.pallas_call(
        functools.partial(early_kernel, groups=groups, group_size=group_size),
        grid=(1,),
        in_specs=[
            smem, lo_spec, q_spec, q_spec, pair_spec, one_spec, pair_spec, kept_spec,
            anywhere, anywhere, anywhere,
        ],
        out_specs=[q_spec, pair_spec, part_spec, part_spec],
        out_shape=[dq_shape, pair, p2_shape, p3_shape],
        input_output_aliases={8: 0, 9: 2, 10: 3},
        cost_estimate=cost,
    )(flags, lo, q, do, kv, e1, e2, kept, dq, p2, p3)
    return dq, a_e, a_l, p2, p3


def on_device(query, keys, values, grad_out, lengths):
    n = lax.axis_size(AXIS)
    me = lax.axis_index(AXIS)
    half_rows = query.shape[2]
    kv_width = keys.shape[3]
    q = query[0]
    do = grad_out[0]
    kv = jnp.concatenate([keys[0], values[0]], axis=2)
    early, late = kv[0], kv[1]
    at_top = me == n - 1
    below_top = me == n - 2

    e1 = shifted(early, 1)
    l1 = shifted(late, -1)
    turn2 = lax.ppermute(early, AXIS, [(n - 1, n - 2), (n - 2, n - 1)])
    turn3 = lax.ppermute(early, AXIS, [(n - 3, n - 1)])
    e2 = shifted(jnp.stack([early, e1]), 2)
    l2 = shifted(jnp.stack([late, jnp.where(at_top, early, l1)]), -2)

    doc_ends = jnp.cumsum(lengths)
    block_ids = jnp.stack([me, 2 * n - 1 - me])
    query_pos = block_ids[:, None] * half_rows + jnp.arange(half_rows, dtype=jnp.int32)[None, :]
    ends = doc_ends[None, None, :]
    doc_start = jnp.max(jnp.where(ends <= query_pos[:, :, None], ends, 0), axis=2)
    lo = (doc_start - (block_ids[:, None] - REACH) * half_rows).astype(jnp.int32)[:, :, None]
    flags = jnp.stack([at_top, below_top]).astype(jnp.int32)

    dq, a_e, a_l, p2, p3 = window_grads(flags, lo, q, do, kv, e1, e2, l1, l2, turn2, turn3)

    zero = jnp.zeros_like(p3[0])
    link = jnp.bfloat16
    a_e = shifted(a_e, -2).astype(jnp.float32)
    back = lax.ppermute(a_l[0], AXIS, [(n - 2, n - 1)]).astype(jnp.float32)
    a_l = shifted(a_l, 2).astype(jnp.float32)
    b_e = shifted((p2[0].astype(jnp.float32) + a_e[1]).astype(link), -1).astype(jnp.float32)
    b_l = shifted((p2[1].astype(jnp.float32) + a_l[1]).astype(link), 1).astype(jnp.float32)
    final_early = p3[0] + a_e[0] + b_e + jnp.where(at_top, a_l[1] + back, zero)
    final_late = p3[1] + a_l[0] + b_l
    final = jnp.stack([final_early, final_late])
    grad_keys = final[:, :, :kv_width].astype(jnp.bfloat16).reshape(keys.shape)
    grad_values = final[:, :, kv_width:].astype(jnp.bfloat16).reshape(values.shape)
    return (dq.reshape(query.shape), grad_keys, grad_values)


def solution(mesh):
    spec = P(AXIS, None, None, None)
    return jax.shard_map(
        on_device,
        mesh=mesh,
        in_specs=(spec, spec, spec, spec, P()),
        out_specs=(spec, spec, spec),
        check_vma=False,
    )
```

```python
import functools
import math

import jax
import jax.numpy as jnp
from jax import lax
from jax.experimental import pallas as pl
from jax.experimental.pallas import tpu as pltpu
from jax.sharding import PartitionSpec as P

HEAD = 128
REACH = 3
AXIS = ("dp", "ctx")


def shifted(value, steps):
    count = lax.axis_size(AXIS)
    pairs = [(s, s + steps) for s in range(count) if 0 <= s + steps < count]
    return lax.ppermute(value, AXIS, pairs)


def window_half(slot, lo_ref, q_ref, do_ref, group_size, emit):
    half_rows = q_ref.shape[1]
    window = 4 * half_rows
    scale = 1.0 / math.sqrt(HEAD)
    lo = lo_ref[0]
    rows = lax.broadcasted_iota(jnp.int32, (half_rows, window), 0)
    cols = lax.broadcasted_iota(jnp.int32, (half_rows, window), 1)
    visible = (cols >= lo) & (cols <= rows + (window - half_rows))
    bias = jnp.where(visible, 0.0, -1e30).astype(jnp.float32)
    bias = jnp.concatenate([bias] * group_size, axis=0)
    nt = (((1,), (1,)), ((), ()))
    tn = (((0,), (0,)), ((), ()))
    qg = jnp.concatenate([q_ref[0, :, h * HEAD:(h + 1) * HEAD] for h in range(group_size)], axis=0)
    dog = jnp.concatenate([do_ref[0, :, h * HEAD:(h + 1) * HEAD] for h in range(group_size)], axis=0)
    kg = jnp.concatenate([slot(j, False) for j in range(4)], axis=0)
    vg = jnp.concatenate([slot(j, True) for j in range(4)], axis=0)
    scores = lax.dot_general(qg, kg, nt, preferred_element_type=jnp.float32) * scale
    masked = scores + bias
    top = jnp.max(masked, axis=1, keepdims=True)
    expd = jnp.exp(masked - top)
    total = jnp.sum(expd, axis=1, keepdims=True)
    probs = (expd * (1.0 / total)).astype(jnp.bfloat16)
    attn = jnp.dot(probs, vg, preferred_element_type=jnp.float32).astype(jnp.bfloat16)
    delta = jnp.sum(dog.astype(jnp.float32) * attn.astype(jnp.float32), axis=1, keepdims=True)
    dprob = lax.dot_general(dog, vg, nt, preferred_element_type=jnp.float32)
    dscore = (probs.astype(jnp.float32) * (dprob - delta) * scale).astype(jnp.bfloat16)
    dq = jnp.dot(dscore, kg, preferred_element_type=jnp.float32).astype(jnp.bfloat16)
    for h in range(group_size):
        emit("dq", h, False, dq[h * half_rows:(h + 1) * half_rows])
    dk = lax.dot_general(dscore, qg, tn, preferred_element_type=jnp.float32)
    dv = lax.dot_general(probs, dog, tn, preferred_element_type=jnp.float32)
    for j in range(4):
        emit("part", j, False, dk[j * half_rows:(j + 1) * half_rows])
        emit("part", j, True, dv[j * half_rows:(j + 1) * half_rows])


def group_cols(is_value):
    groups = pl.num_programs(0)
    lanes = pl.program_id(0) * HEAD + (groups * HEAD if is_value else 0)
    return pl.ds(pl.multiple_of(lanes, HEAD), HEAD)


def late_kernel(
    flags, lo_ref, q_ref, do_ref, kv, l1, l2, turn2, turn3,
    dq_ref, a_l, p2_ref, p3_ref, kept, *, group_size
):
    at_top = flags[0] != 0
    below_top = flags[1] != 0

    def slot(j, is_value):
        cols = group_cols(is_value)
        if j == 0:
            regular = jnp.where(below_top, kv[0, :, cols], l2[1, :, cols])
            return jnp.where(at_top, turn3[:, cols], regular)
        if j == 1:
            return jnp.where(at_top | below_top, turn2[:, cols], l2[0, :, cols])
        if j == 2:
            return jnp.where(at_top, kv[0, :, cols], l1[:, cols])
        return kv[1, :, cols]

    def emit(kind, j, is_value, value):
        if kind == "dq":
            dq_ref[0, :, j * HEAD:(j + 1) * HEAD] = value
            return
        cols = group_cols(is_value)
        if j < 3:
            kept[j, :, cols] = value
        if j == 0:
            a_l[1, :, cols] = value.astype(a_l.dtype)
        elif j == 1:
            a_l[0, :, cols] = value.astype(a_l.dtype)
        elif j == 2:
            p2_ref[0, :, cols] = value.astype(p2_ref.dtype)
        else:
            p3_ref[0, :, cols] = value

    window_half(slot, lo_ref, q_ref, do_ref, group_size, emit)


def early_kernel(
    flags, lo_ref, q_ref, do_ref, kv, e1, e2, kept, dq_in, p2_in, p3_in,
    dq_ref, a_e, p2_ref, p3_ref, *, group_size
):
    del dq_in, p2_in, p3_in
    at_top = flags[0] != 0
    below_top = flags[1] != 0

    def slot(j, is_value):
        cols = group_cols(is_value)
        return (e2[1, :, cols], e2[0, :, cols], e1[:, cols], kv[0, :, cols])[j]

    def emit(kind, j, is_value, value):
        if kind == "dq":
            dq_ref[0, :, j * HEAD:(j + 1) * HEAD] = value
            return
        cols = group_cols(is_value)
        zero = jnp.zeros_like(value)
        if j == 0:
            a_e[1, :, cols] = value.astype(a_e.dtype)
        elif j == 1:
            merged = value + jnp.where(at_top, kept[0, :, cols], zero)
            a_e[0, :, cols] = merged.astype(a_e.dtype)
        elif j == 2:
            merged = value + jnp.where(at_top, kept[1, :, cols], zero)
            p2_ref[0, :, cols] = merged.astype(p2_ref.dtype)
        else:
            merged = (
                value
                + jnp.where(at_top, kept[2, :, cols], zero)
                + jnp.where(below_top, kept[0, :, cols], zero)
            )
            p3_ref[0, :, cols] = merged

    window_half(slot, lo_ref, q_ref, do_ref, group_size, emit)


def window_grads(flags, lo, q, do, kv, e1, e2, l1, l2, turn2, turn3):
    halves, half_rows, width = q.shape
    kv2 = kv.shape[2]
    groups = kv2 // (2 * HEAD)
    group_size = width // (groups * HEAD)
    flops = 6 * 2 * groups * group_size * half_rows * 4 * half_rows * HEAD
    cost = pl.CostEstimate(
        flops=flops,
        transcendentals=groups * group_size * half_rows * 4 * half_rows,
        bytes_accessed=2 * q.size + 6 * kv.size,
    )

    def half_specs(half):
        q_spec = pl.BlockSpec((1, half_rows, width // groups), lambda g: (half, 0, g))
        lo_spec = pl.BlockSpec((1, half_rows, 1), lambda g: (half, 0, 0))
        part_spec = pl.BlockSpec((1, half_rows, kv2), lambda g: (half, 0, 0))
        return q_spec, lo_spec, part_spec

    pair_spec = pl.BlockSpec((2, half_rows, kv2), lambda g: (0, 0, 0))
    one_spec = pl.BlockSpec((half_rows, kv2), lambda g: (0, 0))
    kept_spec = pl.BlockSpec((3, half_rows, kv2), lambda g: (0, 0, 0))
    smem = pl.BlockSpec(memory_space=pltpu.SMEM)
    anywhere = pl.BlockSpec(memory_space=pl.ANY)
    pair = jax.ShapeDtypeStruct((2, half_rows, kv2), jnp.bfloat16)
    dq_shape = jax.ShapeDtypeStruct(q.shape, jnp.bfloat16)
    p2_shape = jax.ShapeDtypeStruct((halves, half_rows, kv2), jnp.bfloat16)
    p3_shape = jax.ShapeDtypeStruct((halves, half_rows, kv2), jnp.float32)

    q_spec, lo_spec, part_spec = half_specs(1)
    dq, a_l, p2, p3, kept = pl.pallas_call(
        functools.partial(late_kernel, group_size=group_size),
        grid=(groups,),
        in_specs=[smem, lo_spec, q_spec, q_spec, pair_spec, one_spec, pair_spec, one_spec, one_spec],
        out_specs=[q_spec, pair_spec, part_spec, part_spec, kept_spec],
        out_shape=[
            dq_shape, pair, p2_shape, p3_shape,
            jax.ShapeDtypeStruct((3, half_rows, kv2), jnp.float32),
        ],
        cost_estimate=cost,
    )(flags, lo, q, do, kv, l1, l2, turn2, turn3)

    q_spec, lo_spec, part_spec = half_specs(0)
    dq, a_e, p2, p3 = pl.pallas_call(
        functools.partial(early_kernel, group_size=group_size),
        grid=(groups,),
        in_specs=[
            smem, lo_spec, q_spec, q_spec, pair_spec, one_spec, pair_spec, kept_spec,
            anywhere, anywhere, anywhere,
        ],
        out_specs=[q_spec, pair_spec, part_spec, part_spec],
        out_shape=[dq_shape, pair, p2_shape, p3_shape],
        input_output_aliases={8: 0, 9: 2, 10: 3},
        cost_estimate=cost,
    )(flags, lo, q, do, kv, e1, e2, kept, dq, p2, p3)
    return dq, a_e, a_l, p2, p3


def on_device(query, keys, values, grad_out, lengths):
    n = lax.axis_size(AXIS)
    me = lax.axis_index(AXIS)
    half_rows = query.shape[2]
    kv_width = keys.shape[3]
    q = query[0]
    do = grad_out[0]
    kv = jnp.concatenate([keys[0], values[0]], axis=2)
    early, late = kv[0], kv[1]
    at_top = me == n - 1
    below_top = me == n - 2

    e1 = shifted(early, 1)
    l1 = shifted(late, -1)
    turn2 = lax.ppermute(early, AXIS, [(n - 1, n - 2), (n - 2, n - 1)])
    turn3 = lax.ppermute(early, AXIS, [(n - 3, n - 1)])
    e2 = shifted(jnp.stack([early, e1]), 2)
    l2 = shifted(jnp.stack([late, jnp.where(at_top, early, l1)]), -2)

    doc_ends = jnp.cumsum(lengths)
    block_ids = jnp.stack([me, 2 * n - 1 - me])
    query_pos = block_ids[:, None] * half_rows + jnp.arange(half_rows, dtype=jnp.int32)[None, :]
    ends = doc_ends[None, None, :]
    doc_start = jnp.max(jnp.where(ends <= query_pos[:, :, None], ends, 0), axis=2)
    lo = (doc_start - (block_ids[:, None] - REACH) * half_rows).astype(jnp.int32)[:, :, None]
    flags = jnp.stack([at_top, below_top]).astype(jnp.int32)

    dq, a_e, a_l, p2, p3 = window_grads(flags, lo, q, do, kv, e1, e2, l1, l2, turn2, turn3)

    zero = jnp.zeros_like(p3[0])
    link = jnp.bfloat16
    a_e = shifted(a_e, -2).astype(jnp.float32)
    back = lax.ppermute(a_l[0], AXIS, [(n - 2, n - 1)]).astype(jnp.float32)
    a_l = shifted(a_l, 2).astype(jnp.float32)
    b_e = shifted((p2[0].astype(jnp.float32) + a_e[1]).astype(link), -1).astype(jnp.float32)
    b_l = shifted((p2[1].astype(jnp.float32) + a_l[1]).astype(link), 1).astype(jnp.float32)
    final_early = p3[0] + a_e[0] + b_e + jnp.where(at_top, a_l[1] + back, zero)
    final_late = p3[1] + a_l[0] + b_l
    final = jnp.stack([final_early, final_late])
    grad_keys = final[:, :, :kv_width].astype(jnp.bfloat16).reshape(keys.shape)
    grad_values = final[:, :, kv_width:].astype(jnp.bfloat16).reshape(values.shape)
    return (dq.reshape(query.shape), grad_keys, grad_values)


def solution(mesh):
    spec = P(AXIS, None, None, None)
    return jax.shard_map(
        on_device,
        mesh=mesh,
        in_specs=(spec, spec, spec, spec, P()),
        out_specs=(spec, spec, spec),
        check_vma=False,
    )
```

```python
import functools
import math

import jax
import jax.numpy as jnp
from jax import lax
from jax.experimental import pallas as pl
from jax.experimental.pallas import tpu as pltpu
from jax.sharding import PartitionSpec as P

HEAD = 128
REACH = 3
AXIS = ("dp", "ctx")


def shifted(value, steps):
    count = lax.axis_size(AXIS)
    pairs = [(s, s + steps) for s in range(count) if 0 <= s + steps < count]
    return lax.ppermute(value, AXIS, pairs)


def window_half(half, slot, lo_ref, q_ref, do_ref, groups, group_size, emit):
    half_rows = q_ref.buf.shape[2]
    window = 4 * half_rows
    kv_width = groups * HEAD
    scale = 1.0 / math.sqrt(HEAD)
    lo = lo_ref[0]
    rows = lax.broadcasted_iota(jnp.int32, (half_rows, window), 0)
    cols = lax.broadcasted_iota(jnp.int32, (half_rows, window), 1)
    visible = (cols >= lo) & (cols <= rows + (window - half_rows))
    bias = jnp.where(visible, 0.0, -1e30).astype(jnp.float32)
    bias = jnp.concatenate([bias] * group_size, axis=0)
    nt = (((1,), (1,)), ((), ()))
    tn = (((0,), (0,)), ((), ()))
    for g in range(groups):
        base = g * group_size * HEAD
        q_ref.wait(g)
        qg = jnp.concatenate(
            [q_ref.buf[0, g, :, h * HEAD:(h + 1) * HEAD] for h in range(group_size)], axis=0
        )
        dog = jnp.concatenate(
            [q_ref.buf[1, g, :, h * HEAD:(h + 1) * HEAD] for h in range(group_size)], axis=0
        )
        kg = jnp.concatenate([slot(j, g * HEAD) for j in range(4)], axis=0)
        vg = jnp.concatenate([slot(j, kv_width + g * HEAD) for j in range(4)], axis=0)
        scores = lax.dot_general(qg, kg, nt, preferred_element_type=jnp.float32) * scale
        masked = scores + bias
        top = jnp.max(masked, axis=1, keepdims=True)
        expd = jnp.exp(masked - top)
        total = jnp.sum(expd, axis=1, keepdims=True)
        probs = (expd * (1.0 / total)).astype(jnp.bfloat16)
        attn = jnp.dot(probs, vg, preferred_element_type=jnp.float32).astype(jnp.bfloat16)
        delta = jnp.sum(dog.astype(jnp.float32) * attn.astype(jnp.float32), axis=1, keepdims=True)
        dprob = lax.dot_general(dog, vg, nt, preferred_element_type=jnp.float32)
        dscore = (probs.astype(jnp.float32) * (dprob - delta) * scale).astype(jnp.bfloat16)
        dq = jnp.dot(dscore, kg, preferred_element_type=jnp.float32).astype(jnp.bfloat16)
        for h in range(group_size):
            emit("dq", h, base + h * HEAD, dq[h * half_rows:(h + 1) * half_rows])
        dk = lax.dot_general(dscore, qg, tn, preferred_element_type=jnp.float32)
        dv = lax.dot_general(probs, dog, tn, preferred_element_type=jnp.float32)
        for j in range(4):
            emit("part", j, g * HEAD, dk[j * half_rows:(j + 1) * half_rows])
            emit("part", j, kv_width + g * HEAD, dv[j * half_rows:(j + 1) * half_rows])


class GroupLoader:
    def __init__(self, half, q_hbm, do_hbm, buf, sems):
        self.buf = buf
        self.copies = []
        width = buf.shape[3]
        for g in range(buf.shape[1]):
            pair = []
            for k, src in enumerate((q_hbm, do_hbm)):
                copy = pltpu.make_async_copy(
                    src.at[half, :, pl.ds(g * width, width)], buf.at[k, g], sems.at[k, g]
                )
                copy.start()
                pair.append(copy)
            self.copies.append(pair)

    def wait(self, g):
        for copy in self.copies[g]:
            copy.wait()


def late_kernel(
    flags, lo_ref, q_hbm, do_hbm, kv, l1, l2, turn2, turn3,
    dq_ref, a_l, p2_ref, p3_ref, kept, buf, sems, *, groups, group_size
):
    q_ref = GroupLoader(1, q_hbm, do_hbm, buf, sems)
    at_top = flags[0] != 0
    below_top = flags[1] != 0

    def slot(j, lanes):
        cols = pl.ds(lanes, HEAD)
        if j == 0:
            regular = jnp.where(below_top, kv[0, :, cols], l2[1, :, cols])
            return jnp.where(at_top, turn3[:, cols], regular)
        if j == 1:
            return jnp.where(at_top | below_top, turn2[:, cols], l2[0, :, cols])
        if j == 2:
            return jnp.where(at_top, kv[0, :, cols], l1[:, cols])
        return kv[1, :, cols]

    def emit(kind, j, lanes, value):
        cols = pl.ds(lanes, HEAD)
        if kind == "dq":
            dq_ref[0, :, cols] = value
            return
        if j < 3:
            kept[j, :, cols] = value
        if j == 0:
            a_l[1, :, cols] = value.astype(a_l.dtype)
        elif j == 1:
            a_l[0, :, cols] = value.astype(a_l.dtype)
        elif j == 2:
            p2_ref[0, :, cols] = value.astype(p2_ref.dtype)
        else:
            p3_ref[0, :, cols] = value

    window_half(1, slot, lo_ref, q_ref, None, groups, group_size, emit)


def early_kernel(
    flags, lo_ref, q_hbm, do_hbm, kv, e1, e2, kept, dq_in, p2_in, p3_in,
    dq_ref, a_e, p2_ref, p3_ref, buf, sems, *, groups, group_size
):
    q_ref = GroupLoader(0, q_hbm, do_hbm, buf, sems)
    del dq_in, p2_in, p3_in
    at_top = flags[0] != 0
    below_top = flags[1] != 0

    def slot(j, lanes):
        cols = pl.ds(lanes, HEAD)
        return (e2[1, :, cols], e2[0, :, cols], e1[:, cols], kv[0, :, cols])[j]

    def emit(kind, j, lanes, value):
        cols = pl.ds(lanes, HEAD)
        if kind == "dq":
            dq_ref[0, :, cols] = value
            return
        zero = jnp.zeros_like(value)
        if j == 0:
            a_e[1, :, cols] = value.astype(a_e.dtype)
        elif j == 1:
            merged = value + jnp.where(at_top, kept[0, :, cols], zero)
            a_e[0, :, cols] = merged.astype(a_e.dtype)
        elif j == 2:
            merged = value + jnp.where(at_top, kept[1, :, cols], zero)
            p2_ref[0, :, cols] = merged.astype(p2_ref.dtype)
        else:
            merged = (
                value
                + jnp.where(at_top, kept[2, :, cols], zero)
                + jnp.where(below_top, kept[0, :, cols], zero)
            )
            p3_ref[0, :, cols] = merged

    window_half(0, slot, lo_ref, q_ref, None, groups, group_size, emit)


def window_grads(flags, lo, q, do, kv, e1, e2, l1, l2, turn2, turn3):
    halves, half_rows, width = q.shape
    kv2 = kv.shape[2]
    groups = kv2 // (2 * HEAD)
    group_size = width // (groups * HEAD)
    flops = 6 * 2 * groups * group_size * half_rows * 4 * half_rows * HEAD
    cost = pl.CostEstimate(
        flops=flops,
        transcendentals=groups * group_size * half_rows * 4 * half_rows,
        bytes_accessed=2 * q.size + 6 * kv.size,
    )

    def half_specs(half):
        q_spec = pl.BlockSpec((1, half_rows, width), lambda s: (half, 0, 0))
        lo_spec = pl.BlockSpec((1, half_rows, 1), lambda s: (half, 0, 0))
        part_spec = pl.BlockSpec((1, half_rows, kv2), lambda s: (half, 0, 0))
        return q_spec, lo_spec, part_spec

    pair_spec = pl.BlockSpec((2, half_rows, kv2), lambda s: (0, 0, 0))
    one_spec = pl.BlockSpec((half_rows, kv2), lambda s: (0, 0))
    kept_spec = pl.BlockSpec((3, half_rows, kv2), lambda s: (0, 0, 0))
    smem = pl.BlockSpec(memory_space=pltpu.SMEM)
    anywhere = pl.BlockSpec(memory_space=pl.ANY)
    pair = jax.ShapeDtypeStruct((2, half_rows, kv2), jnp.bfloat16)
    dq_shape = jax.ShapeDtypeStruct(q.shape, jnp.bfloat16)
    p2_shape = jax.ShapeDtypeStruct((halves, half_rows, kv2), jnp.bfloat16)
    p3_shape = jax.ShapeDtypeStruct((halves, half_rows, kv2), jnp.float32)

    q_spec, lo_spec, part_spec = half_specs(1)
    dq, a_l, p2, p3, kept = pl.pallas_call(
        functools.partial(late_kernel, groups=groups, group_size=group_size),
        grid=(1,),
        in_specs=[smem, lo_spec, anywhere, anywhere, pair_spec, one_spec, pair_spec, one_spec, one_spec],
        out_specs=[q_spec, pair_spec, part_spec, part_spec, kept_spec],
        out_shape=[
            dq_shape, pair, p2_shape, p3_shape,
            jax.ShapeDtypeStruct((3, half_rows, kv2), jnp.float32),
        ],
        scratch_shapes=[
            pltpu.VMEM((2, groups, half_rows, width // groups), jnp.bfloat16),
            pltpu.SemaphoreType.DMA((2, groups)),
        ],
        cost_estimate=cost,
    )(flags, lo, q, do, kv, l1, l2, turn2, turn3)

    q_spec, lo_spec, part_spec = half_specs(0)
    dq, a_e, p2, p3 = pl.pallas_call(
        functools.partial(early_kernel, groups=groups, group_size=group_size),
        grid=(1,),
        in_specs=[
            smem, lo_spec, anywhere, anywhere, pair_spec, one_spec, pair_spec, kept_spec,
            anywhere, anywhere, anywhere,
        ],
        out_specs=[q_spec, pair_spec, part_spec, part_spec],
        out_shape=[dq_shape, pair, p2_shape, p3_shape],
        input_output_aliases={8: 0, 9: 2, 10: 3},
        scratch_shapes=[
            pltpu.VMEM((2, groups, half_rows, width // groups), jnp.bfloat16),
            pltpu.SemaphoreType.DMA((2, groups)),
        ],
        cost_estimate=cost,
    )(flags, lo, q, do, kv, e1, e2, kept, dq, p2, p3)
    return dq, a_e, a_l, p2, p3


def on_device(query, keys, values, grad_out, lengths):
    n = lax.axis_size(AXIS)
    me = lax.axis_index(AXIS)
    half_rows = query.shape[2]
    kv_width = keys.shape[3]
    q = query[0]
    do = grad_out[0]
    kv = jnp.concatenate([keys[0], values[0]], axis=2)
    early, late = kv[0], kv[1]
    at_top = me == n - 1
    below_top = me == n - 2

    e1 = shifted(early, 1)
    l1 = shifted(late, -1)
    turn2 = lax.ppermute(early, AXIS, [(n - 1, n - 2), (n - 2, n - 1)])
    turn3 = lax.ppermute(early, AXIS, [(n - 3, n - 1)])
    e2 = shifted(jnp.stack([early, e1]), 2)
    l2 = shifted(jnp.stack([late, jnp.where(at_top, early, l1)]), -2)

    doc_ends = jnp.cumsum(lengths)
    block_ids = jnp.stack([me, 2 * n - 1 - me])
    query_pos = block_ids[:, None] * half_rows + jnp.arange(half_rows, dtype=jnp.int32)[None, :]
    ends = doc_ends[None, None, :]
    doc_start = jnp.max(jnp.where(ends <= query_pos[:, :, None], ends, 0), axis=2)
    lo = (doc_start - (block_ids[:, None] - REACH) * half_rows).astype(jnp.int32)[:, :, None]
    flags = jnp.stack([at_top, below_top]).astype(jnp.int32)

    dq, a_e, a_l, p2, p3 = window_grads(flags, lo, q, do, kv, e1, e2, l1, l2, turn2, turn3)

    zero = jnp.zeros_like(p3[0])
    link = jnp.bfloat16
    a_e = shifted(a_e, -2).astype(jnp.float32)
    back = lax.ppermute(a_l[0], AXIS, [(n - 2, n - 1)]).astype(jnp.float32)
    a_l = shifted(a_l, 2).astype(jnp.float32)
    b_e = shifted((p2[0].astype(jnp.float32) + a_e[1]).astype(link), -1).astype(jnp.float32)
    b_l = shifted((p2[1].astype(jnp.float32) + a_l[1]).astype(link), 1).astype(jnp.float32)
    final_early = p3[0] + a_e[0] + b_e + jnp.where(at_top, a_l[1] + back, zero)
    final_late = p3[1] + a_l[0] + b_l
    final = jnp.stack([final_early, final_late])
    grad_keys = final[:, :, :kv_width].astype(jnp.bfloat16).reshape(keys.shape)
    grad_values = final[:, :, kv_width:].astype(jnp.bfloat16).reshape(values.shape)
    return (dq.reshape(query.shape), grad_keys, grad_values)


def solution(mesh):
    spec = P(AXIS, None, None, None)
    return jax.shard_map(
        on_device,
        mesh=mesh,
        in_specs=(spec, spec, spec, spec, P()),
        out_specs=(spec, spec, spec),
        check_vma=False,
    )
```

```python
import functools
import math

import jax
import jax.numpy as jnp
from jax import lax
from jax.experimental import pallas as pl
from jax.experimental.pallas import tpu as pltpu
from jax.sharding import PartitionSpec as P

HEAD = 128
REACH = 3
AXIS = ("dp", "ctx")


def shifted(value, steps):
    count = lax.axis_size(AXIS)
    pairs = [(s, s + steps) for s in range(count) if 0 <= s + steps < count]
    return lax.ppermute(value, AXIS, pairs)


def window_half(half, slot, lo_ref, q_ref, do_ref, groups, group_size, emit):
    half_rows = q_ref.shape[1]
    window = 4 * half_rows
    kv_width = groups * HEAD
    scale = 1.0 / math.sqrt(HEAD)
    lo = lo_ref[0]
    rows = lax.broadcasted_iota(jnp.int32, (half_rows, window), 0)
    cols = lax.broadcasted_iota(jnp.int32, (half_rows, window), 1)
    visible = (cols >= lo) & (cols <= rows + (window - half_rows))
    bias = jnp.where(visible, 0.0, -1e30).astype(jnp.float32)
    bias = jnp.concatenate([bias] * group_size, axis=0)
    nt = (((1,), (1,)), ((), ()))
    tn = (((0,), (0,)), ((), ()))
    for g in range(groups):
        base = g * group_size * HEAD
        qg = jnp.concatenate(
            [q_ref[0, :, base + h * HEAD:base + (h + 1) * HEAD] for h in range(group_size)], axis=0
        )
        dog = jnp.concatenate(
            [do_ref[0, :, base + h * HEAD:base + (h + 1) * HEAD] for h in range(group_size)], axis=0
        )
        kg = jnp.concatenate([slot(j, g * HEAD) for j in range(4)], axis=0)
        vg = jnp.concatenate([slot(j, kv_width + g * HEAD) for j in range(4)], axis=0)
        scores = lax.dot_general(qg, kg, nt, preferred_element_type=jnp.float32) * scale
        masked = scores + bias
        top = jnp.max(masked, axis=1, keepdims=True)
        expd = jnp.exp(masked - top)
        total = jnp.sum(expd, axis=1, keepdims=True)
        probs = (expd * (1.0 / total)).astype(jnp.bfloat16)
        attn = jnp.dot(probs, vg, preferred_element_type=jnp.float32).astype(jnp.bfloat16)
        delta = jnp.sum(dog.astype(jnp.float32) * attn.astype(jnp.float32), axis=1, keepdims=True)
        dprob = lax.dot_general(dog, vg, nt, preferred_element_type=jnp.float32)
        dscore = (probs.astype(jnp.float32) * (dprob - delta) * scale).astype(jnp.bfloat16)
        dq = jnp.dot(dscore, kg, preferred_element_type=jnp.float32).astype(jnp.bfloat16)
        for h in range(group_size):
            emit("dq", h, base + h * HEAD, dq[h * half_rows:(h + 1) * half_rows])
        dk = lax.dot_general(dscore, qg, tn, preferred_element_type=jnp.float32)
        dv = lax.dot_general(probs, dog, tn, preferred_element_type=jnp.float32)
        for j in range(4):
            emit("part", j, g * HEAD, dk[j * half_rows:(j + 1) * half_rows])
            emit("part", j, kv_width + g * HEAD, dv[j * half_rows:(j + 1) * half_rows])


def late_kernel(
    flags, lo_ref, q_ref, do_ref, kv, l1, l2, turn2, turn3,
    dq_ref, s0, s1, s2, p3_ref, kept, *, groups, group_size
):
    at_top = flags[0] != 0
    below_top = flags[1] != 0

    def slot(j, lanes):
        cols = pl.ds(lanes, HEAD)
        if j == 0:
            regular = jnp.where(below_top, kv[0, :, cols], l2[1, :, cols])
            return jnp.where(at_top, turn3[:, cols], regular)
        if j == 1:
            return jnp.where(at_top | below_top, turn2[:, cols], l2[0, :, cols])
        if j == 2:
            return jnp.where(at_top, kv[0, :, cols], l1[:, cols])
        return kv[1, :, cols]

    def emit(kind, j, lanes, value):
        cols = pl.ds(lanes, HEAD)
        if kind == "dq":
            dq_ref[0, :, cols] = value
            return
        if j < 3:
            kept[j, :, cols] = value
            (s0, s1, s2)[j][:, cols] = value.astype(s0.dtype)
        else:
            p3_ref[0, :, cols] = value

    window_half(1, slot, lo_ref, q_ref, do_ref, groups, group_size, emit)


def early_kernel(
    flags, lo_ref, q_ref, do_ref, kv, e1, e2, kept, dq_in, p3_in,
    dq_ref, s0, s1, s2, p3_ref, *, groups, group_size
):
    del dq_in, p3_in
    at_top = flags[0] != 0
    below_top = flags[1] != 0

    def slot(j, lanes):
        cols = pl.ds(lanes, HEAD)
        return (e2[1, :, cols], e2[0, :, cols], e1[:, cols], kv[0, :, cols])[j]

    def emit(kind, j, lanes, value):
        cols = pl.ds(lanes, HEAD)
        if kind == "dq":
            dq_ref[0, :, cols] = value
            return
        zero = jnp.zeros_like(value)
        if j == 0:
            s0[:, cols] = value.astype(s0.dtype)
        elif j == 1:
            merged = value + jnp.where(at_top, kept[0, :, cols], zero)
            s1[:, cols] = merged.astype(s1.dtype)
        elif j == 2:
            merged = value + jnp.where(at_top, kept[1, :, cols], zero)
            s2[:, cols] = merged.astype(s2.dtype)
        else:
            merged = (
                value
                + jnp.where(at_top, kept[2, :, cols], zero)
                + jnp.where(below_top, kept[0, :, cols], zero)
            )
            p3_ref[0, :, cols] = merged

    window_half(0, slot, lo_ref, q_ref, do_ref, groups, group_size, emit)


def window_grads(flags, lo, q, do, kv, e1, e2, l1, l2, turn2, turn3):
    halves, half_rows, width = q.shape
    kv2 = kv.shape[2]
    groups = kv2 // (2 * HEAD)
    group_size = width // (groups * HEAD)
    flops = 6 * 2 * groups * group_size * half_rows * 4 * half_rows * HEAD
    cost = pl.CostEstimate(
        flops=flops,
        transcendentals=groups * group_size * half_rows * 4 * half_rows,
        bytes_accessed=2 * q.size + 6 * kv.size,
    )

    def half_specs(half):
        q_spec = pl.BlockSpec((1, half_rows, width), lambda s: (half, 0, 0))
        lo_spec = pl.BlockSpec((1, half_rows, 1), lambda s: (half, 0, 0))
        part_spec = pl.BlockSpec((1, half_rows, kv2), lambda s: (half, 0, 0))
        return q_spec, lo_spec, part_spec

    pair_spec = pl.BlockSpec((2, half_rows, kv2), lambda s: (0, 0, 0))
    one_spec = pl.BlockSpec((half_rows, kv2), lambda s: (0, 0))
    kept_spec = pl.BlockSpec((3, half_rows, kv2), lambda s: (0, 0, 0))
    smem = pl.BlockSpec(memory_space=pltpu.SMEM)
    anywhere = pl.BlockSpec(memory_space=pl.ANY)
    pair = jax.ShapeDtypeStruct((2, half_rows, kv2), jnp.bfloat16)
    dq_shape = jax.ShapeDtypeStruct(q.shape, jnp.bfloat16)
    p2_shape = jax.ShapeDtypeStruct((halves, half_rows, kv2), jnp.bfloat16)
    p3_shape = jax.ShapeDtypeStruct((halves, half_rows, kv2), jnp.float32)

    q_spec, lo_spec, part_spec = half_specs(1)
    slot_shape = jax.ShapeDtypeStruct((half_rows, kv2), jnp.bfloat16)
    dq, l0, l1p, l2p, p3, kept = pl.pallas_call(
        functools.partial(late_kernel, groups=groups, group_size=group_size),
        grid=(1,),
        in_specs=[smem, lo_spec, q_spec, q_spec, pair_spec, one_spec, pair_spec, one_spec, one_spec],
        out_specs=[q_spec, one_spec, one_spec, one_spec, part_spec, kept_spec],
        out_shape=[
            dq_shape, slot_shape, slot_shape, slot_shape, p3_shape,
            jax.ShapeDtypeStruct((3, half_rows, kv2), jnp.float32),
        ],
        cost_estimate=cost,
    )(flags, lo, q, do, kv, l1, l2, turn2, turn3)

    q_spec, lo_spec, part_spec = half_specs(0)
    dq, e0, e1p, e2p, p3 = pl.pallas_call(
        functools.partial(early_kernel, groups=groups, group_size=group_size),
        grid=(1,),
        in_specs=[
            smem, lo_spec, q_spec, q_spec, pair_spec, one_spec, pair_spec, kept_spec,
            anywhere, anywhere,
        ],
        out_specs=[q_spec, one_spec, one_spec, one_spec, part_spec],
        out_shape=[dq_shape, slot_shape, slot_shape, slot_shape, p3_shape],
        input_output_aliases={8: 0, 9: 4},
        cost_estimate=cost,
    )(flags, lo, q, do, kv, e1, e2, kept, dq, p3)
    return dq, (e0, e1p, e2p), (l0, l1p, l2p), p3


def on_device(query, keys, values, grad_out, lengths):
    n = lax.axis_size(AXIS)
    me = lax.axis_index(AXIS)
    half_rows = query.shape[2]
    kv_width = keys.shape[3]
    q = query[0]
    do = grad_out[0]
    kv = jnp.concatenate([keys[0], values[0]], axis=2)
    early, late = kv[0], kv[1]
    at_top = me == n - 1
    below_top = me == n - 2

    e1 = shifted(early, 1)
    l1 = shifted(late, -1)
    turn2 = lax.ppermute(early, AXIS, [(n - 1, n - 2), (n - 2, n - 1)])
    turn3 = lax.ppermute(early, AXIS, [(n - 3, n - 1)])
    e2 = shifted(jnp.stack([early, e1]), 2)
    l2 = shifted(jnp.stack([late, jnp.where(at_top, early, l1)]), -2)

    doc_ends = jnp.cumsum(lengths)
    block_ids = jnp.stack([me, 2 * n - 1 - me])
    query_pos = block_ids[:, None] * half_rows + jnp.arange(half_rows, dtype=jnp.int32)[None, :]
    ends = doc_ends[None, None, :]
    doc_start = jnp.max(jnp.where(ends <= query_pos[:, :, None], ends, 0), axis=2)
    lo = (doc_start - (block_ids[:, None] - REACH) * half_rows).astype(jnp.int32)[:, :, None]
    flags = jnp.stack([at_top, below_top]).astype(jnp.int32)

    dq, early_parts, late_parts, p3 = window_grads(
        flags, lo, q, do, kv, e1, e2, l1, l2, turn2, turn3
    )

    f32 = jnp.float32
    zero = jnp.zeros_like(p3[0])
    from_right = [shifted(early_parts[2 - k], -(k + 1)).astype(f32) for k in range(3)]
    from_left = [shifted(late_parts[2 - k], k + 1).astype(f32) for k in range(3)]
    back2 = lax.ppermute(late_parts[1], AXIS, [(n - 2, n - 1)]).astype(f32)
    back3 = lax.ppermute(late_parts[0], AXIS, [(n - 3, n - 1)]).astype(f32)
    final_early = p3[0] + from_right[0] + from_right[1] + from_right[2] + jnp.where(
        at_top, back2 + back3, zero
    )
    final_late = p3[1] + from_left[0] + from_left[1] + from_left[2]
    final = jnp.stack([final_early, final_late])
    grad_keys = final[:, :, :kv_width].astype(jnp.bfloat16).reshape(keys.shape)
    grad_values = final[:, :, kv_width:].astype(jnp.bfloat16).reshape(values.shape)
    return (dq.reshape(query.shape), grad_keys, grad_values)


def solution(mesh):
    spec = P(AXIS, None, None, None)
    return jax.shard_map(
        on_device,
        mesh=mesh,
        in_specs=(spec, spec, spec, spec, P()),
        out_specs=(spec, spec, spec),
        check_vma=False,
    )
```

```python
import functools
import math

import jax
import jax.numpy as jnp
from jax import lax
from jax.experimental import pallas as pl
from jax.experimental.pallas import tpu as pltpu
from jax.sharding import PartitionSpec as P

HEAD = 128
REACH = 3
AXIS = ("dp", "ctx")


def shifted(value, steps):
    count = lax.axis_size(AXIS)
    pairs = [(s, s + steps) for s in range(count) if 0 <= s + steps < count]
    return lax.ppermute(value, AXIS, pairs)


def window_half(half, slot, lo_ref, q_ref, do_ref, groups, group_size, emit):
    half_rows = q_ref.shape[1]
    window = 4 * half_rows
    kv_width = groups * HEAD
    scale = 1.0 / math.sqrt(HEAD)
    lo = lo_ref[0]
    rows = lax.broadcasted_iota(jnp.int32, (half_rows, window), 0)
    cols = lax.broadcasted_iota(jnp.int32, (half_rows, window), 1)
    visible = (cols >= lo) & (cols <= rows + (window - half_rows))
    bias = jnp.where(visible, 0.0, -1e30).astype(jnp.float32)
    bias = jnp.concatenate([bias] * group_size, axis=0)
    nt = (((1,), (1,)), ((), ()))
    tn = (((0,), (0,)), ((), ()))
    for g in range(groups):
        base = g * group_size * HEAD
        qg = jnp.concatenate(
            [q_ref[0, :, base + h * HEAD:base + (h + 1) * HEAD] for h in range(group_size)], axis=0
        )
        dog = jnp.concatenate(
            [do_ref[0, :, base + h * HEAD:base + (h + 1) * HEAD] for h in range(group_size)], axis=0
        )
        kg = jnp.concatenate([slot(j, g * HEAD) for j in range(4)], axis=0)
        vg = jnp.concatenate([slot(j, kv_width + g * HEAD) for j in range(4)], axis=0)
        scores = lax.dot_general(qg, kg, nt, preferred_element_type=jnp.float32) * scale
        masked = scores + bias
        top = jnp.max(masked, axis=1, keepdims=True)
        expd = jnp.exp(masked - top)
        total = jnp.sum(expd, axis=1, keepdims=True)
        probs = (expd * (1.0 / total)).astype(jnp.bfloat16)
        attn = jnp.dot(probs, vg, preferred_element_type=jnp.float32).astype(jnp.bfloat16)
        delta = jnp.sum(dog.astype(jnp.float32) * attn.astype(jnp.float32), axis=1, keepdims=True)
        dprob = lax.dot_general(dog, vg, nt, preferred_element_type=jnp.float32)
        dscore = (probs.astype(jnp.float32) * (dprob - delta) * scale).astype(jnp.bfloat16)
        dq = jnp.dot(dscore, kg, preferred_element_type=jnp.float32).astype(jnp.bfloat16)
        for h in range(group_size):
            emit("dq", h, base + h * HEAD, dq[h * half_rows:(h + 1) * half_rows])
        dk = lax.dot_general(dscore, qg, tn, preferred_element_type=jnp.float32)
        dv = lax.dot_general(probs, dog, tn, preferred_element_type=jnp.float32)
        for j in range(4):
            emit("part", j, g * HEAD, dk[j * half_rows:(j + 1) * half_rows])
            emit("part", j, kv_width + g * HEAD, dv[j * half_rows:(j + 1) * half_rows])


def late_kernel(
    flags, lo_ref, q_ref, do_ref, kv, l1, l2, turn2, turn3,
    dq_ref, a_l, p2_ref, p3_ref, *, groups, group_size
):
    at_top = flags[0] != 0
    below_top = flags[1] != 0

    def slot(j, lanes):
        cols = pl.ds(lanes, HEAD)
        if j == 0:
            regular = jnp.where(below_top, kv[0, :, cols], l2[1, :, cols])
            return jnp.where(at_top, turn3[:, cols], regular)
        if j == 1:
            return jnp.where(at_top | below_top, turn2[:, cols], l2[0, :, cols])
        if j == 2:
            return jnp.where(at_top, kv[0, :, cols], l1[:, cols])
        return kv[1, :, cols]

    def emit(kind, j, lanes, value):
        cols = pl.ds(lanes, HEAD)
        if kind == "dq":
            dq_ref[0, :, cols] = value
            return
        if j == 0:
            a_l[1, :, cols] = value.astype(a_l.dtype)
        elif j == 1:
            a_l[0, :, cols] = value.astype(a_l.dtype)
        elif j == 2:
            p2_ref[:, cols] = value.astype(p2_ref.dtype)
        else:
            p3_ref[0, :, cols] = value

    window_half(1, slot, lo_ref, q_ref, do_ref, groups, group_size, emit)


def early_kernel(
    flags, lo_ref, q_ref, do_ref, kv, e1, e2, a_l, p2_late, dq_in, p3_in,
    dq_ref, a_e, p2_ref, p3_ref, *, groups, group_size
):
    del dq_in, p3_in
    at_top = flags[0] != 0
    below_top = flags[1] != 0

    def slot(j, lanes):
        cols = pl.ds(lanes, HEAD)
        return (e2[1, :, cols], e2[0, :, cols], e1[:, cols], kv[0, :, cols])[j]

    def emit(kind, j, lanes, value):
        cols = pl.ds(lanes, HEAD)
        if kind == "dq":
            dq_ref[0, :, cols] = value
            return
        zero = jnp.zeros_like(value)
        late0 = a_l[1, :, cols].astype(jnp.float32)
        if j == 0:
            a_e[1, :, cols] = value.astype(a_e.dtype)
        elif j == 1:
            merged = value + jnp.where(at_top, late0, zero)
            a_e[0, :, cols] = merged.astype(a_e.dtype)
        elif j == 2:
            merged = value + jnp.where(at_top, a_l[0, :, cols].astype(jnp.float32), zero)
            p2_ref[:, cols] = merged.astype(p2_ref.dtype)
        else:
            merged = (
                value
                + jnp.where(at_top, p2_late[:, cols].astype(jnp.float32), zero)
                + jnp.where(below_top, late0, zero)
            )
            p3_ref[0, :, cols] = merged

    window_half(0, slot, lo_ref, q_ref, do_ref, groups, group_size, emit)


def window_grads(flags, lo, q, do, kv, e1, e2, l1, l2, turn2, turn3):
    halves, half_rows, width = q.shape
    kv2 = kv.shape[2]
    groups = kv2 // (2 * HEAD)
    group_size = width // (groups * HEAD)
    flops = 6 * 2 * groups * group_size * half_rows * 4 * half_rows * HEAD
    cost = pl.CostEstimate(
        flops=flops,
        transcendentals=groups * group_size * half_rows * 4 * half_rows,
        bytes_accessed=2 * q.size + 6 * kv.size,
    )

    def half_specs(half):
        q_spec = pl.BlockSpec((1, half_rows, width), lambda s: (half, 0, 0))
        lo_spec = pl.BlockSpec((1, half_rows, 1), lambda s: (half, 0, 0))
        part_spec = pl.BlockSpec((1, half_rows, kv2), lambda s: (half, 0, 0))
        return q_spec, lo_spec, part_spec

    pair_spec = pl.BlockSpec((2, half_rows, kv2), lambda s: (0, 0, 0))
    one_spec = pl.BlockSpec((half_rows, kv2), lambda s: (0, 0))
    smem = pl.BlockSpec(memory_space=pltpu.SMEM)
    anywhere = pl.BlockSpec(memory_space=pl.ANY)
    pair = jax.ShapeDtypeStruct((2, half_rows, kv2), jnp.bfloat16)
    dq_shape = jax.ShapeDtypeStruct(q.shape, jnp.bfloat16)
    p2_shape = jax.ShapeDtypeStruct((halves, half_rows, kv2), jnp.bfloat16)
    p3_shape = jax.ShapeDtypeStruct((halves, half_rows, kv2), jnp.float32)

    q_spec, lo_spec, part_spec = half_specs(1)
    slot_shape = jax.ShapeDtypeStruct((half_rows, kv2), jnp.bfloat16)
    dq, a_l, p2_late, p3 = pl.pallas_call(
        functools.partial(late_kernel, groups=groups, group_size=group_size),
        grid=(1,),
        in_specs=[smem, lo_spec, q_spec, q_spec, pair_spec, one_spec, pair_spec, one_spec, one_spec],
        out_specs=[q_spec, pair_spec, one_spec, part_spec],
        out_shape=[dq_shape, pair, slot_shape, p3_shape],
        cost_estimate=cost,
    )(flags, lo, q, do, kv, l1, l2, turn2, turn3)

    q_spec, lo_spec, part_spec = half_specs(0)
    dq, a_e, p2_early, p3 = pl.pallas_call(
        functools.partial(early_kernel, groups=groups, group_size=group_size),
        grid=(1,),
        in_specs=[
            smem, lo_spec, q_spec, q_spec, pair_spec, one_spec, pair_spec, pair_spec, one_spec,
            anywhere, anywhere,
        ],
        out_specs=[q_spec, pair_spec, one_spec, part_spec],
        out_shape=[dq_shape, pair, slot_shape, p3_shape],
        input_output_aliases={9: 0, 10: 3},
        cost_estimate=cost,
    )(flags, lo, q, do, kv, e1, e2, a_l, p2_late, dq, p3)
    return dq, a_e, a_l, (p2_early, p2_late), p3


def on_device(query, keys, values, grad_out, lengths):
    n = lax.axis_size(AXIS)
    me = lax.axis_index(AXIS)
    half_rows = query.shape[2]
    kv_width = keys.shape[3]
    q = query[0]
    do = grad_out[0]
    kv = jnp.concatenate([keys[0], values[0]], axis=2)
    early, late = kv[0], kv[1]
    at_top = me == n - 1
    below_top = me == n - 2

    e1 = shifted(early, 1)
    l1 = shifted(late, -1)
    turn2 = lax.ppermute(early, AXIS, [(n - 1, n - 2), (n - 2, n - 1)])
    turn3 = lax.ppermute(early, AXIS, [(n - 3, n - 1)])
    e2 = shifted(jnp.stack([early, e1]), 2)
    l2 = shifted(jnp.stack([late, jnp.where(at_top, early, l1)]), -2)

    doc_ends = jnp.cumsum(lengths)
    block_ids = jnp.stack([me, 2 * n - 1 - me])
    query_pos = block_ids[:, None] * half_rows + jnp.arange(half_rows, dtype=jnp.int32)[None, :]
    ends = doc_ends[None, None, :]
    doc_start = jnp.max(jnp.where(ends <= query_pos[:, :, None], ends, 0), axis=2)
    lo = (doc_start - (block_ids[:, None] - REACH) * half_rows).astype(jnp.int32)[:, :, None]
    flags = jnp.stack([at_top, below_top]).astype(jnp.int32)

    dq, a_e, a_l, p2, p3 = window_grads(flags, lo, q, do, kv, e1, e2, l1, l2, turn2, turn3)

    zero = jnp.zeros_like(p3[0])
    link = jnp.bfloat16
    a_e = shifted(a_e, -2).astype(jnp.float32)
    back = lax.ppermute(a_l[0], AXIS, [(n - 2, n - 1)]).astype(jnp.float32)
    a_l = shifted(a_l, 2).astype(jnp.float32)
    b_e = shifted((p2[0].astype(jnp.float32) + a_e[1]).astype(link), -1).astype(jnp.float32)
    b_l = shifted((p2[1].astype(jnp.float32) + a_l[1]).astype(link), 1).astype(jnp.float32)
    final_early = p3[0] + a_e[0] + b_e + jnp.where(at_top, a_l[1] + back, zero)
    final_late = p3[1] + a_l[0] + b_l
    final = jnp.stack([final_early, final_late])
    grad_keys = final[:, :, :kv_width].astype(jnp.bfloat16).reshape(keys.shape)
    grad_values = final[:, :, kv_width:].astype(jnp.bfloat16).reshape(values.shape)
    return (dq.reshape(query.shape), grad_keys, grad_values)


def solution(mesh):
    spec = P(AXIS, None, None, None)
    return jax.shard_map(
        on_device,
        mesh=mesh,
        in_specs=(spec, spec, spec, spec, P()),
        out_specs=(spec, spec, spec),
        check_vma=False,
    )
```

```python
import functools
import math

import jax
import jax.numpy as jnp
from jax import lax
from jax.experimental import pallas as pl
from jax.experimental.pallas import tpu as pltpu
from jax.sharding import PartitionSpec as P

HEAD = 128
REACH = 3
AXIS = ("dp", "ctx")


def shifted(value, steps):
    count = lax.axis_size(AXIS)
    pairs = [(s, s + steps) for s in range(count) if 0 <= s + steps < count]
    return lax.ppermute(value, AXIS, pairs)


def window_half(half, slot, lo_ref, q_ref, do_ref, groups, group_size, emit):
    half_rows = q_ref.shape[1]
    window = 4 * half_rows
    kv_width = groups * HEAD
    scale = 1.0 / math.sqrt(HEAD)
    lo = lo_ref[0]
    rows = lax.broadcasted_iota(jnp.int32, (half_rows, window), 0)
    cols = lax.broadcasted_iota(jnp.int32, (half_rows, window), 1)
    visible = (cols >= lo) & (cols <= rows + (window - half_rows))
    bias = jnp.where(visible, 0.0, -1e30).astype(jnp.float32)
    bias = jnp.concatenate([bias] * group_size, axis=0)
    nt = (((1,), (1,)), ((), ()))
    tn = (((0,), (0,)), ((), ()))
    for g in range(groups):
        base = g * group_size * HEAD
        qg = jnp.concatenate(
            [q_ref[0, :, base + h * HEAD:base + (h + 1) * HEAD] for h in range(group_size)], axis=0
        )
        dog = jnp.concatenate(
            [do_ref[0, :, base + h * HEAD:base + (h + 1) * HEAD] for h in range(group_size)], axis=0
        )
        kg = jnp.concatenate([slot(j, g * HEAD) for j in range(4)], axis=0)
        vg = jnp.concatenate([slot(j, kv_width + g * HEAD) for j in range(4)], axis=0)
        scores = lax.dot_general(qg, kg, nt, preferred_element_type=jnp.float32) * scale
        masked = scores + bias
        top = jnp.max(masked, axis=1, keepdims=True)
        expd = jnp.exp(masked - top)
        total = jnp.sum(expd, axis=1, keepdims=True)
        probs = (expd * (1.0 / total)).astype(jnp.bfloat16)
        attn = jnp.dot(probs, vg, preferred_element_type=jnp.float32).astype(jnp.bfloat16)
        delta = jnp.sum(dog.astype(jnp.float32) * attn.astype(jnp.float32), axis=1, keepdims=True)
        dprob = lax.dot_general(dog, vg, nt, preferred_element_type=jnp.float32)
        dscore = (probs.astype(jnp.float32) * (dprob - delta) * scale).astype(jnp.bfloat16)
        dq = jnp.dot(dscore, kg, preferred_element_type=jnp.float32).astype(jnp.bfloat16)
        for h in range(group_size):
            emit("dq", h, base + h * HEAD, dq[h * half_rows:(h + 1) * half_rows])
        dk = lax.dot_general(dscore, qg, tn, preferred_element_type=jnp.float32)
        dv = lax.dot_general(probs, dog, tn, preferred_element_type=jnp.float32)
        for j in range(4):
            emit("part", j, g * HEAD, dk[j * half_rows:(j + 1) * half_rows])
            emit("part", j, kv_width + g * HEAD, dv[j * half_rows:(j + 1) * half_rows])


def late_kernel(
    flags, lo_ref, q_ref, do_ref, kv, l1, l2, turn2, turn3,
    dq_ref, a_l, p2_ref, p3_ref, *, groups, group_size
):
    at_top = flags[0] != 0
    below_top = flags[1] != 0

    def slot(j, lanes):
        cols = pl.ds(lanes, HEAD)
        if j == 0:
            regular = jnp.where(below_top, kv[0, :, cols], l2[1, :, cols])
            return jnp.where(at_top, turn3[:, cols], regular)
        if j == 1:
            return jnp.where(at_top | below_top, turn2[:, cols], l2[0, :, cols])
        if j == 2:
            return jnp.where(at_top, kv[0, :, cols], l1[:, cols])
        return kv[1, :, cols]

    def emit(kind, j, lanes, value):
        cols = pl.ds(lanes, HEAD)
        if kind == "dq":
            dq_ref[0, :, cols] = value
            return
        if j == 0:
            a_l[1, :, cols] = value.astype(a_l.dtype)
        elif j == 1:
            a_l[0, :, cols] = value.astype(a_l.dtype)
        elif j == 2:
            p2_ref[:, cols] = value.astype(p2_ref.dtype)
        else:
            p3_ref[0, :, cols] = value

    window_half(1, slot, lo_ref, q_ref, do_ref, groups, group_size, emit)


def early_kernel(
    flags, lo_ref, q_ref, do_ref, kv, e1, e2, a_l, p2_late, dq_in, p3_in,
    dq_ref, a_e, p2_ref, p3_ref, *, groups, group_size
):
    del dq_in, p3_in
    at_top = flags[0] != 0
    below_top = flags[1] != 0

    def slot(j, lanes):
        cols = pl.ds(lanes, HEAD)
        return (e2[1, :, cols], e2[0, :, cols], e1[:, cols], kv[0, :, cols])[j]

    def emit(kind, j, lanes, value):
        cols = pl.ds(lanes, HEAD)
        if kind == "dq":
            dq_ref[0, :, cols] = value
            return
        zero = jnp.zeros_like(value)
        late0 = a_l[1, :, cols].astype(jnp.float32)
        if j == 0:
            a_e[1, :, cols] = value.astype(a_e.dtype)
        elif j == 1:
            merged = value + jnp.where(at_top, late0, zero)
            a_e[0, :, cols] = merged.astype(a_e.dtype)
        elif j == 2:
            merged = value + jnp.where(at_top, a_l[0, :, cols].astype(jnp.float32), zero)
            p2_ref[:, cols] = merged.astype(p2_ref.dtype)
        else:
            merged = (
                value
                + jnp.where(at_top, p2_late[:, cols].astype(jnp.float32), zero)
                + jnp.where(below_top, late0, zero)
            )
            p3_ref[0, :, cols] = merged

    window_half(0, slot, lo_ref, q_ref, do_ref, groups, group_size, emit)


def window_grads(flags, lo, q, do, kv, e1, e2, l1, l2, turn2, turn3, between):
    halves, half_rows, width = q.shape
    kv2 = kv.shape[2]
    groups = kv2 // (2 * HEAD)
    group_size = width // (groups * HEAD)
    flops = 6 * 2 * groups * group_size * half_rows * 4 * half_rows * HEAD
    cost = pl.CostEstimate(
        flops=flops,
        transcendentals=groups * group_size * half_rows * 4 * half_rows,
        bytes_accessed=2 * q.size + 6 * kv.size,
    )

    def half_specs(half):
        q_spec = pl.BlockSpec((1, half_rows, width), lambda s: (half, 0, 0))
        lo_spec = pl.BlockSpec((1, half_rows, 1), lambda s: (half, 0, 0))
        part_spec = pl.BlockSpec((1, half_rows, kv2), lambda s: (half, 0, 0))
        return q_spec, lo_spec, part_spec

    pair_spec = pl.BlockSpec((2, half_rows, kv2), lambda s: (0, 0, 0))
    one_spec = pl.BlockSpec((half_rows, kv2), lambda s: (0, 0))
    smem = pl.BlockSpec(memory_space=pltpu.SMEM)
    anywhere = pl.BlockSpec(memory_space=pl.ANY)
    pair = jax.ShapeDtypeStruct((2, half_rows, kv2), jnp.bfloat16)
    dq_shape = jax.ShapeDtypeStruct(q.shape, jnp.bfloat16)
    p2_shape = jax.ShapeDtypeStruct((halves, half_rows, kv2), jnp.bfloat16)
    p3_shape = jax.ShapeDtypeStruct((halves, half_rows, kv2), jnp.float32)

    q_spec, lo_spec, part_spec = half_specs(1)
    slot_shape = jax.ShapeDtypeStruct((half_rows, kv2), jnp.bfloat16)
    dq, a_l, p2_late, p3 = pl.pallas_call(
        functools.partial(late_kernel, groups=groups, group_size=group_size),
        grid=(1,),
        in_specs=[smem, lo_spec, q_spec, q_spec, pair_spec, one_spec, pair_spec, one_spec, one_spec],
        out_specs=[q_spec, pair_spec, one_spec, part_spec],
        out_shape=[dq_shape, pair, slot_shape, p3_shape],
        cost_estimate=cost,
    )(flags, lo, q, do, kv, l1, l2, turn2, turn3)

    q_spec, lo_spec, part_spec = half_specs(0)
    q, extra = lax.optimization_barrier((q, between(a_l, p2_late)))
    dq, a_e, p2_early, p3 = pl.pallas_call(
        functools.partial(early_kernel, groups=groups, group_size=group_size),
        grid=(1,),
        in_specs=[
            smem, lo_spec, q_spec, q_spec, pair_spec, one_spec, pair_spec, pair_spec, one_spec,
            anywhere, anywhere,
        ],
        out_specs=[q_spec, pair_spec, one_spec, part_spec],
        out_shape=[dq_shape, pair, slot_shape, p3_shape],
        input_output_aliases={9: 0, 10: 3},
        cost_estimate=cost,
    )(flags, lo, q, do, kv, e1, e2, a_l, p2_late, dq, p3)
    return dq, a_e, extra, p2_early, p3


def on_device(query, keys, values, grad_out, lengths):
    n = lax.axis_size(AXIS)
    me = lax.axis_index(AXIS)
    half_rows = query.shape[2]
    kv_width = keys.shape[3]
    q = query[0]
    do = grad_out[0]
    kv = jnp.concatenate([keys[0], values[0]], axis=2)
    early, late = kv[0], kv[1]
    at_top = me == n - 1
    below_top = me == n - 2

    e1 = shifted(early, 1)
    l1 = shifted(late, -1)
    turn2 = lax.ppermute(early, AXIS, [(n - 1, n - 2), (n - 2, n - 1)])
    turn3 = lax.ppermute(early, AXIS, [(n - 3, n - 1)])
    e2 = shifted(jnp.stack([early, e1]), 2)
    l2 = shifted(jnp.stack([late, jnp.where(at_top, early, l1)]), -2)

    doc_ends = jnp.cumsum(lengths)
    block_ids = jnp.stack([me, 2 * n - 1 - me])
    query_pos = block_ids[:, None] * half_rows + jnp.arange(half_rows, dtype=jnp.int32)[None, :]
    ends = doc_ends[None, None, :]
    doc_start = jnp.max(jnp.where(ends <= query_pos[:, :, None], ends, 0), axis=2)
    lo = (doc_start - (block_ids[:, None] - REACH) * half_rows).astype(jnp.int32)[:, :, None]
    flags = jnp.stack([at_top, below_top]).astype(jnp.int32)

    link = jnp.bfloat16
    f32 = jnp.float32

    def late_return(a_l, p2_late):
        back = lax.ppermute(a_l[0], AXIS, [(n - 2, n - 1)]).astype(f32)
        a_l = shifted(a_l, 2).astype(f32)
        b_l = shifted((p2_late.astype(f32) + a_l[1]).astype(link), 1).astype(f32)
        return a_l, b_l, back

    dq, a_e, (a_l, b_l, back), p2_early, p3 = window_grads(
        flags, lo, q, do, kv, e1, e2, l1, l2, turn2, turn3, late_return
    )

    zero = jnp.zeros_like(p3[0])
    a_e = shifted(a_e, -2).astype(f32)
    b_e = shifted((p2_early.astype(f32) + a_e[1]).astype(link), -1).astype(f32)
    final_early = p3[0] + a_e[0] + b_e + jnp.where(at_top, a_l[1] + back, zero)
    final_late = p3[1] + a_l[0] + b_l
    final = jnp.stack([final_early, final_late])
    grad_keys = final[:, :, :kv_width].astype(jnp.bfloat16).reshape(keys.shape)
    grad_values = final[:, :, kv_width:].astype(jnp.bfloat16).reshape(values.shape)
    return (dq.reshape(query.shape), grad_keys, grad_values)


def solution(mesh):
    spec = P(AXIS, None, None, None)
    return jax.shard_map(
        on_device,
        mesh=mesh,
        in_specs=(spec, spec, spec, spec, P()),
        out_specs=(spec, spec, spec),
        check_vma=False,
    )
```

```python
import functools
import math

import jax
import jax.numpy as jnp
from jax import lax
from jax.experimental import pallas as pl
from jax.experimental.pallas import tpu as pltpu
from jax.sharding import PartitionSpec as P

HEAD = 128
REACH = 3
AXIS = ("dp", "ctx")


def shifted(value, steps):
    count = lax.axis_size(AXIS)
    pairs = [(s, s + steps) for s in range(count) if 0 <= s + steps < count]
    return lax.ppermute(value, AXIS, pairs)


def window_half(half, slot, lo_ref, q_ref, do_ref, groups, group_size, emit):
    half_rows = q_ref.shape[1]
    window = 4 * half_rows
    kv_width = groups * HEAD
    scale = 1.0 / math.sqrt(HEAD)
    lo = lo_ref[0]
    rows = lax.broadcasted_iota(jnp.int32, (half_rows, window), 0)
    cols = lax.broadcasted_iota(jnp.int32, (half_rows, window), 1)
    visible = (cols >= lo) & (cols <= rows + (window - half_rows))
    bias = jnp.where(visible, 0.0, -1e30).astype(jnp.float32)
    bias = jnp.concatenate([bias] * group_size, axis=0)
    nt = (((1,), (1,)), ((), ()))
    tn = (((0,), (0,)), ((), ()))
    for g in range(groups):
        base = g * group_size * HEAD
        qg = jnp.concatenate(
            [q_ref[0, :, base + h * HEAD:base + (h + 1) * HEAD] for h in range(group_size)], axis=0
        )
        dog = jnp.concatenate(
            [do_ref[0, :, base + h * HEAD:base + (h + 1) * HEAD] for h in range(group_size)], axis=0
        )
        kg = jnp.concatenate([slot(j, g * HEAD) for j in range(4)], axis=0)
        vg = jnp.concatenate([slot(j, kv_width + g * HEAD) for j in range(4)], axis=0)
        scores = lax.dot_general(qg, kg, nt, preferred_element_type=jnp.float32) * scale
        masked = scores + bias
        top = jnp.max(masked, axis=1, keepdims=True)
        expd = jnp.exp(masked - top)
        total = jnp.sum(expd, axis=1, keepdims=True)
        probs = (expd * (1.0 / total)).astype(jnp.bfloat16)
        attn = jnp.dot(probs, vg, preferred_element_type=jnp.float32).astype(jnp.bfloat16)
        delta = jnp.sum(dog.astype(jnp.float32) * attn.astype(jnp.float32), axis=1, keepdims=True)
        dprob = lax.dot_general(dog, vg, nt, preferred_element_type=jnp.float32)
        dscore = (probs.astype(jnp.float32) * (dprob - delta) * scale).astype(jnp.bfloat16)
        dq = jnp.dot(dscore, kg, preferred_element_type=jnp.float32).astype(jnp.bfloat16)
        for h in range(group_size):
            emit("dq", h, base + h * HEAD, dq[h * half_rows:(h + 1) * half_rows])
        dk = lax.dot_general(dscore, qg, tn, preferred_element_type=jnp.float32)
        dv = lax.dot_general(probs, dog, tn, preferred_element_type=jnp.float32)
        for j in range(4):
            emit("part", j, g * HEAD, dk[j * half_rows:(j + 1) * half_rows])
            emit("part", j, kv_width + g * HEAD, dv[j * half_rows:(j + 1) * half_rows])


class OwnBlocks:
    def __init__(self, keys, values):
        self.keys = keys
        self.values = values

    def __getitem__(self, index):
        half, rows, cols = index
        width = self.keys.shape[2]
        if cols.start >= width:
            return self.values[half, rows, pl.ds(cols.start - width, cols.size)]
        return self.keys[half, rows, cols]


def late_kernel(
    flags, lo_ref, q_ref, do_ref, keys, values, l1, l2, turn2, turn3,
    dq_ref, a_l, p2_ref, p3_ref, *, groups, group_size
):
    at_top = flags[0] != 0
    below_top = flags[1] != 0
    kv = OwnBlocks(keys, values)

    def slot(j, lanes):
        cols = pl.ds(lanes, HEAD)
        if j == 0:
            regular = jnp.where(below_top, kv[0, :, cols], l2[1, :, cols])
            return jnp.where(at_top, turn3[:, cols], regular)
        if j == 1:
            return jnp.where(at_top | below_top, turn2[:, cols], l2[0, :, cols])
        if j == 2:
            return jnp.where(at_top, kv[0, :, cols], l1[:, cols])
        return kv[1, :, cols]

    def emit(kind, j, lanes, value):
        cols = pl.ds(lanes, HEAD)
        if kind == "dq":
            dq_ref[0, :, cols] = value
            return
        if j == 0:
            a_l[1, :, cols] = value.astype(a_l.dtype)
        elif j == 1:
            a_l[0, :, cols] = value.astype(a_l.dtype)
        elif j == 2:
            p2_ref[:, cols] = value.astype(p2_ref.dtype)
        else:
            p3_ref[0, :, cols] = value

    window_half(1, slot, lo_ref, q_ref, do_ref, groups, group_size, emit)


def early_kernel(
    flags, lo_ref, q_ref, do_ref, keys, values, e1, e2, a_l, p2_late, dq_in, p3_in,
    dq_ref, a_e, p2_ref, p3_ref, *, groups, group_size
):
    del dq_in, p3_in
    at_top = flags[0] != 0
    below_top = flags[1] != 0
    kv = OwnBlocks(keys, values)

    def slot(j, lanes):
        cols = pl.ds(lanes, HEAD)
        return (e2[1, :, cols], e2[0, :, cols], e1[:, cols], kv[0, :, cols])[j]

    def emit(kind, j, lanes, value):
        cols = pl.ds(lanes, HEAD)
        if kind == "dq":
            dq_ref[0, :, cols] = value
            return
        zero = jnp.zeros_like(value)
        late0 = a_l[1, :, cols].astype(jnp.float32)
        if j == 0:
            a_e[1, :, cols] = value.astype(a_e.dtype)
        elif j == 1:
            merged = value + jnp.where(at_top, late0, zero)
            a_e[0, :, cols] = merged.astype(a_e.dtype)
        elif j == 2:
            merged = value + jnp.where(at_top, a_l[0, :, cols].astype(jnp.float32), zero)
            p2_ref[:, cols] = merged.astype(p2_ref.dtype)
        else:
            merged = (
                value
                + jnp.where(at_top, p2_late[:, cols].astype(jnp.float32), zero)
                + jnp.where(below_top, late0, zero)
            )
            p3_ref[0, :, cols] = merged

    window_half(0, slot, lo_ref, q_ref, do_ref, groups, group_size, emit)


def window_grads(flags, lo, q, do, keys, values, e1, e2, l1, l2, turn2, turn3):
    halves, half_rows, width = q.shape
    kv2 = 2 * keys.shape[2]
    groups = kv2 // (2 * HEAD)
    group_size = width // (groups * HEAD)
    flops = 6 * 2 * groups * group_size * half_rows * 4 * half_rows * HEAD
    cost = pl.CostEstimate(
        flops=flops,
        transcendentals=groups * group_size * half_rows * 4 * half_rows,
        bytes_accessed=2 * q.size + 12 * keys.size,
    )

    def half_specs(half):
        q_spec = pl.BlockSpec((1, half_rows, width), lambda s: (half, 0, 0))
        lo_spec = pl.BlockSpec((1, half_rows, 1), lambda s: (half, 0, 0))
        part_spec = pl.BlockSpec((1, half_rows, kv2), lambda s: (half, 0, 0))
        return q_spec, lo_spec, part_spec

    pair_spec = pl.BlockSpec((2, half_rows, kv2), lambda s: (0, 0, 0))
    own_spec = pl.BlockSpec((2, half_rows, kv2 // 2), lambda s: (0, 0, 0))
    one_spec = pl.BlockSpec((half_rows, kv2), lambda s: (0, 0))
    smem = pl.BlockSpec(memory_space=pltpu.SMEM)
    anywhere = pl.BlockSpec(memory_space=pl.ANY)
    pair = jax.ShapeDtypeStruct((2, half_rows, kv2), jnp.bfloat16)
    dq_shape = jax.ShapeDtypeStruct(q.shape, jnp.bfloat16)
    p2_shape = jax.ShapeDtypeStruct((halves, half_rows, kv2), jnp.bfloat16)
    p3_shape = jax.ShapeDtypeStruct((halves, half_rows, kv2), jnp.float32)

    q_spec, lo_spec, part_spec = half_specs(1)
    slot_shape = jax.ShapeDtypeStruct((half_rows, kv2), jnp.bfloat16)
    dq, a_l, p2_late, p3 = pl.pallas_call(
        functools.partial(late_kernel, groups=groups, group_size=group_size),
        grid=(1,),
        in_specs=[smem, lo_spec, q_spec, q_spec, own_spec, own_spec, one_spec, pair_spec, one_spec, one_spec],
        out_specs=[q_spec, pair_spec, one_spec, part_spec],
        out_shape=[dq_shape, pair, slot_shape, p3_shape],
        cost_estimate=cost,
    )(flags, lo, q, do, keys, values, l1, l2, turn2, turn3)

    q_spec, lo_spec, part_spec = half_specs(0)
    dq, a_e, p2_early, p3 = pl.pallas_call(
        functools.partial(early_kernel, groups=groups, group_size=group_size),
        grid=(1,),
        in_specs=[
            smem, lo_spec, q_spec, q_spec, own_spec, own_spec, one_spec, pair_spec, pair_spec, one_spec,
            anywhere, anywhere,
        ],
        out_specs=[q_spec, pair_spec, one_spec, part_spec],
        out_shape=[dq_shape, pair, slot_shape, p3_shape],
        input_output_aliases={10: 0, 11: 3},
        cost_estimate=cost,
    )(flags, lo, q, do, keys, values, e1, e2, a_l, p2_late, dq, p3)
    return dq, a_e, a_l, (p2_early, p2_late), p3


def on_device(query, keys, values, grad_out, lengths):
    n = lax.axis_size(AXIS)
    me = lax.axis_index(AXIS)
    half_rows = query.shape[2]
    kv_width = keys.shape[3]
    q = query[0]
    do = grad_out[0]
    kv = jnp.concatenate([keys[0], values[0]], axis=2)
    early, late = kv[0], kv[1]
    at_top = me == n - 1
    below_top = me == n - 2

    e1 = shifted(early, 1)
    l1 = shifted(late, -1)
    turn2 = lax.ppermute(early, AXIS, [(n - 1, n - 2), (n - 2, n - 1)])
    turn3 = lax.ppermute(early, AXIS, [(n - 3, n - 1)])
    e2 = shifted(jnp.stack([early, e1]), 2)
    l2 = shifted(jnp.stack([late, jnp.where(at_top, early, l1)]), -2)

    doc_ends = jnp.cumsum(lengths)
    block_ids = jnp.stack([me, 2 * n - 1 - me])
    query_pos = block_ids[:, None] * half_rows + jnp.arange(half_rows, dtype=jnp.int32)[None, :]
    ends = doc_ends[None, None, :]
    doc_start = jnp.max(jnp.where(ends <= query_pos[:, :, None], ends, 0), axis=2)
    lo = (doc_start - (block_ids[:, None] - REACH) * half_rows).astype(jnp.int32)[:, :, None]
    flags = jnp.stack([at_top, below_top]).astype(jnp.int32)

    dq, a_e, a_l, p2, p3 = window_grads(flags, lo, q, do, keys[0], values[0], e1, e2, l1, l2, turn2, turn3)

    zero = jnp.zeros_like(p3[0])
    link = jnp.bfloat16
    a_e = shifted(a_e, -2).astype(jnp.float32)
    back = lax.ppermute(a_l[0], AXIS, [(n - 2, n - 1)]).astype(jnp.float32)
    a_l = shifted(a_l, 2).astype(jnp.float32)
    b_e = shifted((p2[0].astype(jnp.float32) + a_e[1]).astype(link), -1).astype(jnp.float32)
    b_l = shifted((p2[1].astype(jnp.float32) + a_l[1]).astype(link), 1).astype(jnp.float32)
    final_early = p3[0] + a_e[0] + b_e + jnp.where(at_top, a_l[1] + back, zero)
    final_late = p3[1] + a_l[0] + b_l
    final = jnp.stack([final_early, final_late])
    grad_keys = final[:, :, :kv_width].astype(jnp.bfloat16).reshape(keys.shape)
    grad_values = final[:, :, kv_width:].astype(jnp.bfloat16).reshape(values.shape)
    return (dq.reshape(query.shape), grad_keys, grad_values)


def solution(mesh):
    spec = P(AXIS, None, None, None)
    return jax.shard_map(
        on_device,
        mesh=mesh,
        in_specs=(spec, spec, spec, spec, P()),
        out_specs=(spec, spec, spec),
        check_vma=False,
    )
```

```python
import functools
import math

import jax
import jax.numpy as jnp
from jax import lax
from jax.experimental import pallas as pl
from jax.experimental.pallas import tpu as pltpu
from jax.sharding import PartitionSpec as P

HEAD = 128
REACH = 3
AXIS = ("dp", "ctx")


def shifted(value, steps):
    count = lax.axis_size(AXIS)
    pairs = [(s, s + steps) for s in range(count) if 0 <= s + steps < count]
    return lax.ppermute(value, AXIS, pairs)


def window_half(half, slot, lo_ref, q_ref, do_ref, groups, group_size, emit):
    half_rows = q_ref.shape[1]
    window = 4 * half_rows
    kv_width = groups * HEAD
    scale = 1.0 / math.sqrt(HEAD)
    block = lo_ref.block(half)
    ends = lo_ref.ends[...]
    query_pos = block * half_rows + lax.broadcasted_iota(jnp.int32, (half_rows, ends.shape[1]), 0)
    doc_start = jnp.max(jnp.where(ends <= query_pos, ends, 0), axis=1, keepdims=True)
    lo = doc_start - (block - REACH) * half_rows
    rows = lax.broadcasted_iota(jnp.int32, (half_rows, window), 0)
    cols = lax.broadcasted_iota(jnp.int32, (half_rows, window), 1)
    visible = (cols >= lo) & (cols <= rows + (window - half_rows))
    bias = jnp.where(visible, 0.0, -1e30).astype(jnp.float32)
    bias = jnp.concatenate([bias] * group_size, axis=0)
    nt = (((1,), (1,)), ((), ()))
    tn = (((0,), (0,)), ((), ()))
    for g in range(groups):
        base = g * group_size * HEAD
        qg = jnp.concatenate(
            [q_ref[0, :, base + h * HEAD:base + (h + 1) * HEAD] for h in range(group_size)], axis=0
        )
        dog = jnp.concatenate(
            [do_ref[0, :, base + h * HEAD:base + (h + 1) * HEAD] for h in range(group_size)], axis=0
        )
        kg = jnp.concatenate([slot(j, g * HEAD) for j in range(4)], axis=0)
        vg = jnp.concatenate([slot(j, kv_width + g * HEAD) for j in range(4)], axis=0)
        scores = lax.dot_general(qg, kg, nt, preferred_element_type=jnp.float32) * scale
        masked = scores + bias
        top = jnp.max(masked, axis=1, keepdims=True)
        expd = jnp.exp(masked - top)
        total = jnp.sum(expd, axis=1, keepdims=True)
        probs = (expd * (1.0 / total)).astype(jnp.bfloat16)
        attn = jnp.dot(probs, vg, preferred_element_type=jnp.float32).astype(jnp.bfloat16)
        delta = jnp.sum(dog.astype(jnp.float32) * attn.astype(jnp.float32), axis=1, keepdims=True)
        dprob = lax.dot_general(dog, vg, nt, preferred_element_type=jnp.float32)
        dscore = (probs.astype(jnp.float32) * (dprob - delta) * scale).astype(jnp.bfloat16)
        dq = jnp.dot(dscore, kg, preferred_element_type=jnp.float32).astype(jnp.bfloat16)
        for h in range(group_size):
            emit("dq", h, base + h * HEAD, dq[h * half_rows:(h + 1) * half_rows])
        dk = lax.dot_general(dscore, qg, tn, preferred_element_type=jnp.float32)
        dv = lax.dot_general(probs, dog, tn, preferred_element_type=jnp.float32)
        for j in range(4):
            emit("part", j, g * HEAD, dk[j * half_rows:(j + 1) * half_rows])
            emit("part", j, kv_width + g * HEAD, dv[j * half_rows:(j + 1) * half_rows])


class DocBounds:
    def __init__(self, flags, ends):
        self.flags = flags
        self.ends = ends

    def block(self, half):
        return self.flags[2 + half]


class OwnBlocks:
    def __init__(self, keys, values):
        self.keys = keys
        self.values = values

    def __getitem__(self, index):
        half, rows, cols = index
        width = self.keys.shape[2]
        if cols.start >= width:
            return self.values[half, rows, pl.ds(cols.start - width, cols.size)]
        return self.keys[half, rows, cols]


def late_kernel(
    flags, ends_ref, q_ref, do_ref, keys, values, l1, l2, turn2, turn3,
    dq_ref, a_l, p2_ref, p3_ref, *, groups, group_size
):
    lo_ref = DocBounds(flags, ends_ref)
    at_top = flags[0] != 0
    below_top = flags[1] != 0
    kv = OwnBlocks(keys, values)

    def slot(j, lanes):
        cols = pl.ds(lanes, HEAD)
        if j == 0:
            regular = jnp.where(below_top, kv[0, :, cols], l2[1, :, cols])
            return jnp.where(at_top, turn3[:, cols], regular)
        if j == 1:
            return jnp.where(at_top | below_top, turn2[:, cols], l2[0, :, cols])
        if j == 2:
            return jnp.where(at_top, kv[0, :, cols], l1[:, cols])
        return kv[1, :, cols]

    def emit(kind, j, lanes, value):
        cols = pl.ds(lanes, HEAD)
        if kind == "dq":
            dq_ref[0, :, cols] = value
            return
        if j == 0:
            a_l[1, :, cols] = value.astype(a_l.dtype)
        elif j == 1:
            a_l[0, :, cols] = value.astype(a_l.dtype)
        elif j == 2:
            p2_ref[:, cols] = value.astype(p2_ref.dtype)
        else:
            p3_ref[0, :, cols] = value

    window_half(1, slot, lo_ref, q_ref, do_ref, groups, group_size, emit)


def early_kernel(
    flags, ends_ref, q_ref, do_ref, keys, values, e1, e2, a_l, p2_late, dq_in, p3_in,
    dq_ref, a_e, p2_ref, p3_ref, *, groups, group_size
):
    lo_ref = DocBounds(flags, ends_ref)
    del dq_in, p3_in
    at_top = flags[0] != 0
    below_top = flags[1] != 0
    kv = OwnBlocks(keys, values)

    def slot(j, lanes):
        cols = pl.ds(lanes, HEAD)
        return (e2[1, :, cols], e2[0, :, cols], e1[:, cols], kv[0, :, cols])[j]

    def emit(kind, j, lanes, value):
        cols = pl.ds(lanes, HEAD)
        if kind == "dq":
            dq_ref[0, :, cols] = value
            return
        zero = jnp.zeros_like(value)
        late0 = a_l[1, :, cols].astype(jnp.float32)
        if j == 0:
            a_e[1, :, cols] = value.astype(a_e.dtype)
        elif j == 1:
            merged = value + jnp.where(at_top, late0, zero)
            a_e[0, :, cols] = merged.astype(a_e.dtype)
        elif j == 2:
            merged = value + jnp.where(at_top, a_l[0, :, cols].astype(jnp.float32), zero)
            p2_ref[:, cols] = merged.astype(p2_ref.dtype)
        else:
            merged = (
                value
                + jnp.where(at_top, p2_late[:, cols].astype(jnp.float32), zero)
                + jnp.where(below_top, late0, zero)
            )
            p3_ref[0, :, cols] = merged

    window_half(0, slot, lo_ref, q_ref, do_ref, groups, group_size, emit)


def window_grads(flags, lo, q, do, keys, values, e1, e2, l1, l2, turn2, turn3):
    halves, half_rows, width = q.shape
    kv2 = 2 * keys.shape[2]
    groups = kv2 // (2 * HEAD)
    group_size = width // (groups * HEAD)
    flops = 6 * 2 * groups * group_size * half_rows * 4 * half_rows * HEAD
    cost = pl.CostEstimate(
        flops=flops,
        transcendentals=groups * group_size * half_rows * 4 * half_rows,
        bytes_accessed=2 * q.size + 12 * keys.size,
    )

    def half_specs(half):
        q_spec = pl.BlockSpec((1, half_rows, width), lambda s: (half, 0, 0))
        lo_spec = pl.BlockSpec(lo.shape, lambda s: (0, 0))
        part_spec = pl.BlockSpec((1, half_rows, kv2), lambda s: (half, 0, 0))
        return q_spec, lo_spec, part_spec

    pair_spec = pl.BlockSpec((2, half_rows, kv2), lambda s: (0, 0, 0))
    own_spec = pl.BlockSpec((2, half_rows, kv2 // 2), lambda s: (0, 0, 0))
    one_spec = pl.BlockSpec((half_rows, kv2), lambda s: (0, 0))
    smem = pl.BlockSpec(memory_space=pltpu.SMEM)
    anywhere = pl.BlockSpec(memory_space=pl.ANY)
    pair = jax.ShapeDtypeStruct((2, half_rows, kv2), jnp.bfloat16)
    dq_shape = jax.ShapeDtypeStruct(q.shape, jnp.bfloat16)
    p2_shape = jax.ShapeDtypeStruct((halves, half_rows, kv2), jnp.bfloat16)
    p3_shape = jax.ShapeDtypeStruct((halves, half_rows, kv2), jnp.float32)

    q_spec, lo_spec, part_spec = half_specs(1)
    slot_shape = jax.ShapeDtypeStruct((half_rows, kv2), jnp.bfloat16)
    dq, a_l, p2_late, p3 = pl.pallas_call(
        functools.partial(late_kernel, groups=groups, group_size=group_size),
        grid=(1,),
        in_specs=[smem, lo_spec, q_spec, q_spec, own_spec, own_spec, one_spec, pair_spec, one_spec, one_spec],
        out_specs=[q_spec, pair_spec, one_spec, part_spec],
        out_shape=[dq_shape, pair, slot_shape, p3_shape],
        cost_estimate=cost,
    )(flags, lo, q, do, keys, values, l1, l2, turn2, turn3)

    q_spec, lo_spec, part_spec = half_specs(0)
    dq, a_e, p2_early, p3 = pl.pallas_call(
        functools.partial(early_kernel, groups=groups, group_size=group_size),
        grid=(1,),
        in_specs=[
            smem, lo_spec, q_spec, q_spec, own_spec, own_spec, one_spec, pair_spec, pair_spec, one_spec,
            anywhere, anywhere,
        ],
        out_specs=[q_spec, pair_spec, one_spec, part_spec],
        out_shape=[dq_shape, pair, slot_shape, p3_shape],
        input_output_aliases={10: 0, 11: 3},
        cost_estimate=cost,
    )(flags, lo, q, do, keys, values, e1, e2, a_l, p2_late, dq, p3)
    return dq, a_e, a_l, (p2_early, p2_late), p3


def on_device(query, keys, values, grad_out, lengths):
    n = lax.axis_size(AXIS)
    me = lax.axis_index(AXIS)
    half_rows = query.shape[2]
    kv_width = keys.shape[3]
    q = query[0]
    do = grad_out[0]
    kv = jnp.concatenate([keys[0], values[0]], axis=2)
    early, late = kv[0], kv[1]
    at_top = me == n - 1
    below_top = me == n - 2

    e1 = shifted(early, 1)
    l1 = shifted(late, -1)
    turn2 = lax.ppermute(early, AXIS, [(n - 1, n - 2), (n - 2, n - 1)])
    turn3 = lax.ppermute(early, AXIS, [(n - 3, n - 1)])
    e2 = shifted(jnp.stack([early, e1]), 2)
    l2 = shifted(jnp.stack([late, jnp.where(at_top, early, l1)]), -2)

    lo = jnp.cumsum(lengths).astype(jnp.int32)[None, :]
    flags = jnp.stack([at_top, below_top, me, 2 * n - 1 - me]).astype(jnp.int32)

    dq, a_e, a_l, p2, p3 = window_grads(flags, lo, q, do, keys[0], values[0], e1, e2, l1, l2, turn2, turn3)

    zero = jnp.zeros_like(p3[0])
    link = jnp.bfloat16
    a_e = shifted(a_e, -2).astype(jnp.float32)
    back = lax.ppermute(a_l[0], AXIS, [(n - 2, n - 1)]).astype(jnp.float32)
    a_l = shifted(a_l, 2).astype(jnp.float32)
    b_e = shifted((p2[0].astype(jnp.float32) + a_e[1]).astype(link), -1).astype(jnp.float32)
    b_l = shifted((p2[1].astype(jnp.float32) + a_l[1]).astype(link), 1).astype(jnp.float32)
    final_early = p3[0] + a_e[0] + b_e + jnp.where(at_top, a_l[1] + back, zero)
    final_late = p3[1] + a_l[0] + b_l
    final = jnp.stack([final_early, final_late])
    grad_keys = final[:, :, :kv_width].astype(jnp.bfloat16).reshape(keys.shape)
    grad_values = final[:, :, kv_width:].astype(jnp.bfloat16).reshape(values.shape)
    return (dq.reshape(query.shape), grad_keys, grad_values)


def solution(mesh):
    spec = P(AXIS, None, None, None)
    return jax.shard_map(
        on_device,
        mesh=mesh,
        in_specs=(spec, spec, spec, spec, P()),
        out_specs=(spec, spec, spec),
        check_vma=False,
    )
```

```python
import functools
import math

import jax
import jax.numpy as jnp
from jax import lax
from jax.experimental import pallas as pl
from jax.experimental.pallas import tpu as pltpu
from jax.sharding import PartitionSpec as P

HEAD = 128
REACH = 3
AXIS = ("dp", "ctx")


def shifted(value, steps):
    count = lax.axis_size(AXIS)
    pairs = [(s, s + steps) for s in range(count) if 0 <= s + steps < count]
    return lax.ppermute(value, AXIS, pairs)


def window_half(half, slot, lo_ref, q_ref, do_ref, groups, group_size, emit):
    half_rows = q_ref.shape[1]
    window = 4 * half_rows
    kv_width = groups * HEAD
    scale = 1.0 / math.sqrt(HEAD)
    block = lo_ref.block(half)
    ends = lo_ref.ends[...]
    query_pos = block * half_rows + lax.broadcasted_iota(jnp.int32, (half_rows, ends.shape[1]), 0)
    doc_start = jnp.max(jnp.where(ends <= query_pos, ends, 0), axis=1, keepdims=True)
    lo = doc_start - (block - REACH) * half_rows
    rows = lax.broadcasted_iota(jnp.int32, (half_rows, window), 0)
    cols = lax.broadcasted_iota(jnp.int32, (half_rows, window), 1)
    visible = (cols >= lo) & (cols <= rows + (window - half_rows))
    bias = jnp.where(visible, 0.0, -1e30).astype(jnp.float32)
    bias = jnp.concatenate([bias] * group_size, axis=0)
    nt = (((1,), (1,)), ((), ()))
    tn = (((0,), (0,)), ((), ()))
    for g in range(groups):
        base = g * group_size * HEAD
        qg = jnp.concatenate(
            [q_ref[0, :, base + h * HEAD:base + (h + 1) * HEAD] for h in range(group_size)], axis=0
        )
        dog = jnp.concatenate(
            [do_ref[0, :, base + h * HEAD:base + (h + 1) * HEAD] for h in range(group_size)], axis=0
        )
        kg = jnp.concatenate([slot(j, g * HEAD) for j in range(4)], axis=0)
        vg = jnp.concatenate([slot(j, kv_width + g * HEAD) for j in range(4)], axis=0)
        scores = lax.dot_general(qg, kg, nt, preferred_element_type=jnp.float32) * scale
        masked = scores + bias
        top = jnp.max(masked, axis=1, keepdims=True)
        expd = jnp.exp(masked - top)
        total = jnp.sum(expd, axis=1, keepdims=True)
        probs = (expd * (1.0 / total)).astype(jnp.bfloat16)
        attn = jnp.dot(probs, vg, preferred_element_type=jnp.float32).astype(jnp.bfloat16)
        delta = jnp.sum(dog.astype(jnp.float32) * attn.astype(jnp.float32), axis=1, keepdims=True)
        dprob = lax.dot_general(dog, vg, nt, preferred_element_type=jnp.float32)
        dscore = (probs.astype(jnp.float32) * (dprob - delta) * scale).astype(jnp.bfloat16)
        dq = jnp.dot(dscore, kg, preferred_element_type=jnp.float32).astype(jnp.bfloat16)
        for h in range(group_size):
            emit("dq", h, base + h * HEAD, dq[h * half_rows:(h + 1) * half_rows])
        dk = lax.dot_general(dscore, qg, tn, preferred_element_type=jnp.float32)
        dv = lax.dot_general(probs, dog, tn, preferred_element_type=jnp.float32)
        for j in range(4):
            emit("part", j, g * HEAD, dk[j * half_rows:(j + 1) * half_rows])
            emit("part", j, kv_width + g * HEAD, dv[j * half_rows:(j + 1) * half_rows])


class DocBounds:
    def __init__(self, flags, ends):
        self.flags = flags
        self.ends = ends

    def block(self, half):
        return self.flags[2 + half]


class OwnBlocks:
    def __init__(self, keys, values):
        self.keys = keys
        self.values = values

    def __getitem__(self, index):
        half, rows, cols = index
        width = self.keys.shape[2]
        if cols.start >= width:
            return self.values[half, rows, pl.ds(cols.start - width, cols.size)]
        return self.keys[half, rows, cols]


def late_kernel(
    flags, ends_ref, q_ref, do_ref, keys, values, l1, l2, turn2, turn3,
    dq_ref, a_l, p2_ref, p3_ref, *, groups, group_size
):
    lo_ref = DocBounds(flags, ends_ref)
    at_top = flags[0] != 0
    below_top = flags[1] != 0
    kv = OwnBlocks(keys, values)

    def slot(j, lanes):
        cols = pl.ds(lanes, HEAD)
        if j == 0:
            regular = jnp.where(below_top, kv[0, :, cols], l2[1, :, cols])
            return jnp.where(at_top, turn3[:, cols], regular)
        if j == 1:
            return jnp.where(at_top | below_top, turn2[:, cols], l2[0, :, cols])
        if j == 2:
            return jnp.where(at_top, kv[0, :, cols], l1[:, cols])
        return kv[1, :, cols]

    def emit(kind, j, lanes, value):
        cols = pl.ds(lanes, HEAD)
        if kind == "dq":
            dq_ref[0, :, cols] = value
            return
        if j == 0:
            a_l[1, :, cols] = value.astype(a_l.dtype)
        elif j == 1:
            a_l[0, :, cols] = value.astype(a_l.dtype)
        elif j == 2:
            p2_ref[:, cols] = value.astype(p2_ref.dtype)
        else:
            p3_ref[0, :, cols] = value

    window_half(1, slot, lo_ref, q_ref, do_ref, groups, group_size, emit)


def early_kernel(
    flags, ends_ref, q_ref, do_ref, keys, values, e1, e2, a_l, p2_late, dq_in, p3_in,
    dq_ref, a_e, p2_ref, p3_ref, *, groups, group_size
):
    lo_ref = DocBounds(flags, ends_ref)
    del dq_in, p3_in
    at_top = flags[0] != 0
    below_top = flags[1] != 0
    kv = OwnBlocks(keys, values)

    def slot(j, lanes):
        cols = pl.ds(lanes, HEAD)
        return (e2[1, :, cols], e2[0, :, cols], e1[:, cols], kv[0, :, cols])[j]

    def emit(kind, j, lanes, value):
        cols = pl.ds(lanes, HEAD)
        if kind == "dq":
            dq_ref[0, :, cols] = value
            return
        zero = jnp.zeros_like(value)
        late0 = a_l[1, :, cols].astype(jnp.float32)
        if j == 0:
            a_e[1, :, cols] = value.astype(a_e.dtype)
        elif j == 1:
            merged = value + jnp.where(at_top, late0, zero)
            a_e[0, :, cols] = merged.astype(a_e.dtype)
        elif j == 2:
            merged = value + jnp.where(at_top, a_l[0, :, cols].astype(jnp.float32), zero)
            p2_ref[:, cols] = merged.astype(p2_ref.dtype)
        else:
            merged = (
                value
                + jnp.where(at_top, p2_late[:, cols].astype(jnp.float32), zero)
                + jnp.where(below_top, late0, zero)
            )
            p3_ref[0, :, cols] = merged

    window_half(0, slot, lo_ref, q_ref, do_ref, groups, group_size, emit)


def window_grads(flags, lo, q, do, keys, values, e1, e2, l1, l2, turn2, turn3):
    halves, half_rows, width = q.shape
    kv2 = 2 * keys.shape[2]
    groups = kv2 // (2 * HEAD)
    group_size = width // (groups * HEAD)
    flops = 6 * 2 * groups * group_size * half_rows * 4 * half_rows * HEAD
    cost = pl.CostEstimate(
        flops=flops,
        transcendentals=groups * group_size * half_rows * 4 * half_rows,
        bytes_accessed=2 * q.size + 12 * keys.size,
    )

    def half_specs(half):
        q_spec = pl.BlockSpec((1, half_rows, width), lambda s: (half, 0, 0))
        lo_spec = pl.BlockSpec(lo.shape, lambda s: (0, 0))
        part_spec = pl.BlockSpec((1, half_rows, kv2), lambda s: (half, 0, 0))
        return q_spec, lo_spec, part_spec

    pair_spec = pl.BlockSpec((2, half_rows, kv2), lambda s: (0, 0, 0))
    own_spec = pl.BlockSpec((2, half_rows, kv2 // 2), lambda s: (0, 0, 0))
    one_spec = pl.BlockSpec((half_rows, kv2), lambda s: (0, 0))
    smem = pl.BlockSpec(memory_space=pltpu.SMEM)
    anywhere = pl.BlockSpec(memory_space=pl.ANY)
    pair = jax.ShapeDtypeStruct((2, half_rows, kv2), jnp.bfloat16)
    dq_shape = jax.ShapeDtypeStruct(q.shape, jnp.bfloat16)
    p2_shape = jax.ShapeDtypeStruct((halves, half_rows, kv2), jnp.bfloat16)
    p3_shape = jax.ShapeDtypeStruct((halves, half_rows, kv2), jnp.float32)

    q_spec, lo_spec, part_spec = half_specs(1)
    slot_shape = jax.ShapeDtypeStruct((half_rows, kv2), jnp.bfloat16)
    dq, a_l, p2_late, p3 = pl.pallas_call(
        functools.partial(late_kernel, groups=groups, group_size=group_size),
        grid=(1,),
        in_specs=[smem, lo_spec, q_spec, q_spec, own_spec, own_spec, one_spec, pair_spec, one_spec, one_spec],
        out_specs=[q_spec, pair_spec, one_spec, part_spec],
        out_shape=[dq_shape, pair, slot_shape, p3_shape],
        cost_estimate=cost,
    )(flags, lo, q, do, keys, values, l1, l2, turn2, turn3)

    q_spec, lo_spec, part_spec = half_specs(0)
    dq, a_e, p2_early, p3 = pl.pallas_call(
        functools.partial(early_kernel, groups=groups, group_size=group_size),
        grid=(1,),
        in_specs=[
            smem, lo_spec, q_spec, q_spec, own_spec, own_spec, one_spec, pair_spec, pair_spec, one_spec,
            anywhere, anywhere,
        ],
        out_specs=[q_spec, pair_spec, one_spec, part_spec],
        out_shape=[dq_shape, pair, slot_shape, p3_shape],
        input_output_aliases={10: 0, 11: 3},
        cost_estimate=cost,
    )(flags, lo, q, do, keys, values, e1, e2, a_l, p2_late, dq, p3)
    return dq, a_e, a_l, (p2_early, p2_late), p3


def on_device(query, keys, values, grad_out, lengths):
    n = lax.axis_size(AXIS)
    me = lax.axis_index(AXIS)
    half_rows = query.shape[2]
    kv_width = keys.shape[3]
    q = query[0]
    do = grad_out[0]
    kv = jnp.concatenate([keys[0], values[0]], axis=2)
    early, late = kv[0], kv[1]
    at_top = me == n - 1
    below_top = me == n - 2

    even = me % 2 == 0
    first = lax.ppermute(
        jnp.where(even, early, late), AXIS,
        [(s, s ^ 1) for s in range(n)],
    )
    second = lax.ppermute(
        jnp.where(even, late, early), AXIS,
        [(s, s + 1 if s % 2 else s - 1) for s in range(1, n - 1)],
    )
    e1 = jnp.where(even, second, first)
    l1 = jnp.where(even, first, second)
    turn2 = lax.ppermute(early, AXIS, [(n - 1, n - 2), (n - 2, n - 1)])
    turn3 = lax.ppermute(early, AXIS, [(n - 3, n - 1)])
    e2 = shifted(jnp.stack([early, e1]), 2)
    l2 = shifted(jnp.stack([late, jnp.where(at_top, early, l1)]), -2)

    lo = jnp.cumsum(lengths).astype(jnp.int32)[None, :]
    flags = jnp.stack([at_top, below_top, me, 2 * n - 1 - me]).astype(jnp.int32)

    dq, a_e, a_l, p2, p3 = window_grads(flags, lo, q, do, keys[0], values[0], e1, e2, l1, l2, turn2, turn3)

    zero = jnp.zeros_like(p3[0])
    link = jnp.bfloat16
    a_e = shifted(a_e, -2).astype(jnp.float32)
    back = lax.ppermute(a_l[0], AXIS, [(n - 2, n - 1)]).astype(jnp.float32)
    a_l = shifted(a_l, 2).astype(jnp.float32)
    b_e = shifted((p2[0].astype(jnp.float32) + a_e[1]).astype(link), -1).astype(jnp.float32)
    b_l = shifted((p2[1].astype(jnp.float32) + a_l[1]).astype(link), 1).astype(jnp.float32)
    final_early = p3[0] + a_e[0] + b_e + jnp.where(at_top, a_l[1] + back, zero)
    final_late = p3[1] + a_l[0] + b_l
    final = jnp.stack([final_early, final_late])
    grad_keys = final[:, :, :kv_width].astype(jnp.bfloat16).reshape(keys.shape)
    grad_values = final[:, :, kv_width:].astype(jnp.bfloat16).reshape(values.shape)
    return (dq.reshape(query.shape), grad_keys, grad_values)


def solution(mesh):
    spec = P(AXIS, None, None, None)
    return jax.shard_map(
        on_device,
        mesh=mesh,
        in_specs=(spec, spec, spec, spec, P()),
        out_specs=(spec, spec, spec),
        check_vma=False,
    )
```

```python
import functools
import math

import jax
import jax.numpy as jnp
from jax import lax
from jax.experimental import pallas as pl
from jax.experimental.pallas import tpu as pltpu
from jax.sharding import PartitionSpec as P

HEAD = 128
REACH = 3
AXIS = ("dp", "ctx")


def shifted(value, steps):
    count = lax.axis_size(AXIS)
    pairs = [(s, s + steps) for s in range(count) if 0 <= s + steps < count]
    return lax.ppermute(value, AXIS, pairs)


def window_half(half, slot, lo_ref, q_ref, do_ref, groups, group_size, emit):
    half_rows = q_ref.shape[1]
    window = 4 * half_rows
    kv_width = groups * HEAD
    scale = 1.0 / math.sqrt(HEAD)
    block = lo_ref.block(half)
    ends = lo_ref.ends[...]
    query_pos = block * half_rows + lax.broadcasted_iota(jnp.int32, (half_rows, ends.shape[1]), 0)
    doc_start = jnp.max(jnp.where(ends <= query_pos, ends, 0), axis=1, keepdims=True)
    lo = doc_start - (block - REACH) * half_rows
    rows = lax.broadcasted_iota(jnp.int32, (half_rows, window), 0)
    cols = lax.broadcasted_iota(jnp.int32, (half_rows, window), 1)
    visible = (cols >= lo) & (cols <= rows + (window - half_rows))
    bias = jnp.where(visible, 0.0, -1e30).astype(jnp.float32)
    bias = jnp.concatenate([bias] * group_size, axis=0)
    nt = (((1,), (1,)), ((), ()))
    for g in range(groups):
        base = g * group_size * HEAD
        qg = jnp.concatenate(
            [q_ref[0, :, base + h * HEAD:base + (h + 1) * HEAD] for h in range(group_size)], axis=0
        )
        dog = jnp.concatenate(
            [do_ref[0, :, base + h * HEAD:base + (h + 1) * HEAD] for h in range(group_size)], axis=0
        )
        kg = jnp.concatenate([slot(j, g * HEAD) for j in range(4)], axis=0)
        vg = jnp.concatenate([slot(j, kv_width + g * HEAD) for j in range(4)], axis=0)
        scores = lax.dot_general(qg, kg, nt, preferred_element_type=jnp.float32) * scale
        masked = scores + bias
        top = jnp.max(masked, axis=1, keepdims=True)
        expd = jnp.exp(masked - top)
        total = jnp.sum(expd, axis=1, keepdims=True)
        probs = (expd * (1.0 / total)).astype(jnp.bfloat16)
        attn = jnp.dot(probs, vg, preferred_element_type=jnp.float32).astype(jnp.bfloat16)
        delta = jnp.sum(dog.astype(jnp.float32) * attn.astype(jnp.float32), axis=1, keepdims=True)
        dprob = lax.dot_general(dog, vg, nt, preferred_element_type=jnp.float32)
        dscore = (probs.astype(jnp.float32) * (dprob - delta) * scale).astype(jnp.bfloat16)
        dq = jnp.dot(dscore, kg, preferred_element_type=jnp.float32).astype(jnp.bfloat16)
        for h in range(group_size):
            emit("dq", h, base + h * HEAD, dq[h * half_rows:(h + 1) * half_rows])
        dk = jnp.dot(qg.T, dscore, preferred_element_type=jnp.float32).T
        dv = jnp.dot(dog.T, probs, preferred_element_type=jnp.float32).T
        for j in range(4):
            emit("part", j, g * HEAD, dk[j * half_rows:(j + 1) * half_rows])
            emit("part", j, kv_width + g * HEAD, dv[j * half_rows:(j + 1) * half_rows])


class DocBounds:
    def __init__(self, flags, ends):
        self.flags = flags
        self.ends = ends

    def block(self, half):
        return self.flags[2 + half]


class OwnBlocks:
    def __init__(self, keys, values):
        self.keys = keys
        self.values = values

    def __getitem__(self, index):
        half, rows, cols = index
        width = self.keys.shape[2]
        if cols.start >= width:
            return self.values[half, rows, pl.ds(cols.start - width, cols.size)]
        return self.keys[half, rows, cols]


def late_kernel(
    flags, ends_ref, q_ref, do_ref, keys, values, l1, l2, turn2, turn3,
    dq_ref, a_l, p2_ref, p3_ref, *, groups, group_size
):
    lo_ref = DocBounds(flags, ends_ref)
    at_top = flags[0] != 0
    below_top = flags[1] != 0
    kv = OwnBlocks(keys, values)

    def slot(j, lanes):
        cols = pl.ds(lanes, HEAD)
        if j == 0:
            regular = jnp.where(below_top, kv[0, :, cols], l2[1, :, cols])
            return jnp.where(at_top, turn3[:, cols], regular)
        if j == 1:
            return jnp.where(at_top | below_top, turn2[:, cols], l2[0, :, cols])
        if j == 2:
            return jnp.where(at_top, kv[0, :, cols], l1[:, cols])
        return kv[1, :, cols]

    def emit(kind, j, lanes, value):
        cols = pl.ds(lanes, HEAD)
        if kind == "dq":
            dq_ref[0, :, cols] = value
            return
        if j == 0:
            a_l[1, :, cols] = value.astype(a_l.dtype)
        elif j == 1:
            a_l[0, :, cols] = value.astype(a_l.dtype)
        elif j == 2:
            p2_ref[:, cols] = value.astype(p2_ref.dtype)
        else:
            p3_ref[0, :, cols] = value

    window_half(1, slot, lo_ref, q_ref, do_ref, groups, group_size, emit)


def early_kernel(
    flags, ends_ref, q_ref, do_ref, keys, values, e1, e2, a_l, p2_late, dq_in, p3_in,
    dq_ref, a_e, p2_ref, p3_ref, *, groups, group_size
):
    lo_ref = DocBounds(flags, ends_ref)
    del dq_in, p3_in
    at_top = flags[0] != 0
    below_top = flags[1] != 0
    kv = OwnBlocks(keys, values)

    def slot(j, lanes):
        cols = pl.ds(lanes, HEAD)
        return (e2[1, :, cols], e2[0, :, cols], e1[:, cols], kv[0, :, cols])[j]

    def emit(kind, j, lanes, value):
        cols = pl.ds(lanes, HEAD)
        if kind == "dq":
            dq_ref[0, :, cols] = value
            return
        zero = jnp.zeros_like(value)
        late0 = a_l[1, :, cols].astype(jnp.float32)
        if j == 0:
            a_e[1, :, cols] = value.astype(a_e.dtype)
        elif j == 1:
            merged = value + jnp.where(at_top, late0, zero)
            a_e[0, :, cols] = merged.astype(a_e.dtype)
        elif j == 2:
            merged = value + jnp.where(at_top, a_l[0, :, cols].astype(jnp.float32), zero)
            p2_ref[:, cols] = merged.astype(p2_ref.dtype)
        else:
            merged = (
                value
                + jnp.where(at_top, p2_late[:, cols].astype(jnp.float32), zero)
                + jnp.where(below_top, late0, zero)
            )
            p3_ref[0, :, cols] = merged

    window_half(0, slot, lo_ref, q_ref, do_ref, groups, group_size, emit)


def window_grads(flags, lo, q, do, keys, values, e1, e2, l1, l2, turn2, turn3):
    halves, half_rows, width = q.shape
    kv2 = 2 * keys.shape[2]
    groups = kv2 // (2 * HEAD)
    group_size = width // (groups * HEAD)
    flops = 6 * 2 * groups * group_size * half_rows * 4 * half_rows * HEAD
    cost = pl.CostEstimate(
        flops=flops,
        transcendentals=groups * group_size * half_rows * 4 * half_rows,
        bytes_accessed=2 * q.size + 12 * keys.size,
    )

    def half_specs(half):
        q_spec = pl.BlockSpec((1, half_rows, width), lambda s: (half, 0, 0))
        lo_spec = pl.BlockSpec(lo.shape, lambda s: (0, 0))
        part_spec = pl.BlockSpec((1, half_rows, kv2), lambda s: (half, 0, 0))
        return q_spec, lo_spec, part_spec

    pair_spec = pl.BlockSpec((2, half_rows, kv2), lambda s: (0, 0, 0))
    own_spec = pl.BlockSpec((2, half_rows, kv2 // 2), lambda s: (0, 0, 0))
    one_spec = pl.BlockSpec((half_rows, kv2), lambda s: (0, 0))
    smem = pl.BlockSpec(memory_space=pltpu.SMEM)
    anywhere = pl.BlockSpec(memory_space=pl.ANY)
    pair = jax.ShapeDtypeStruct((2, half_rows, kv2), jnp.bfloat16)
    dq_shape = jax.ShapeDtypeStruct(q.shape, jnp.bfloat16)
    p2_shape = jax.ShapeDtypeStruct((halves, half_rows, kv2), jnp.bfloat16)
    p3_shape = jax.ShapeDtypeStruct((halves, half_rows, kv2), jnp.float32)

    q_spec, lo_spec, part_spec = half_specs(1)
    slot_shape = jax.ShapeDtypeStruct((half_rows, kv2), jnp.bfloat16)
    dq, a_l, p2_late, p3 = pl.pallas_call(
        functools.partial(late_kernel, groups=groups, group_size=group_size),
        grid=(1,),
        in_specs=[smem, lo_spec, q_spec, q_spec, own_spec, own_spec, one_spec, pair_spec, one_spec, one_spec],
        out_specs=[q_spec, pair_spec, one_spec, part_spec],
        out_shape=[dq_shape, pair, slot_shape, p3_shape],
        cost_estimate=cost,
    )(flags, lo, q, do, keys, values, l1, l2, turn2, turn3)

    q_spec, lo_spec, part_spec = half_specs(0)
    dq, a_e, p2_early, p3 = pl.pallas_call(
        functools.partial(early_kernel, groups=groups, group_size=group_size),
        grid=(1,),
        in_specs=[
            smem, lo_spec, q_spec, q_spec, own_spec, own_spec, one_spec, pair_spec, pair_spec, one_spec,
            anywhere, anywhere,
        ],
        out_specs=[q_spec, pair_spec, one_spec, part_spec],
        out_shape=[dq_shape, pair, slot_shape, p3_shape],
        input_output_aliases={10: 0, 11: 3},
        cost_estimate=cost,
    )(flags, lo, q, do, keys, values, e1, e2, a_l, p2_late, dq, p3)
    return dq, a_e, a_l, (p2_early, p2_late), p3


def on_device(query, keys, values, grad_out, lengths):
    n = lax.axis_size(AXIS)
    me = lax.axis_index(AXIS)
    half_rows = query.shape[2]
    kv_width = keys.shape[3]
    q = query[0]
    do = grad_out[0]
    kv = jnp.concatenate([keys[0], values[0]], axis=2)
    early, late = kv[0], kv[1]
    at_top = me == n - 1
    below_top = me == n - 2

    e1 = shifted(early, 1)
    l1 = shifted(late, -1)
    turn2 = lax.ppermute(early, AXIS, [(n - 1, n - 2), (n - 2, n - 1)])
    turn3 = lax.ppermute(early, AXIS, [(n - 3, n - 1)])
    e2 = shifted(jnp.stack([early, e1]), 2)
    l2 = shifted(jnp.stack([late, jnp.where(at_top, early, l1)]), -2)

    lo = jnp.cumsum(lengths).astype(jnp.int32)[None, :]
    flags = jnp.stack([at_top, below_top, me, 2 * n - 1 - me]).astype(jnp.int32)

    dq, a_e, a_l, p2, p3 = window_grads(flags, lo, q, do, keys[0], values[0], e1, e2, l1, l2, turn2, turn3)

    zero = jnp.zeros_like(p3[0])
    link = jnp.bfloat16
    a_e = shifted(a_e, -2).astype(jnp.float32)
    back = lax.ppermute(a_l[0], AXIS, [(n - 2, n - 1)]).astype(jnp.float32)
    a_l = shifted(a_l, 2).astype(jnp.float32)
    b_e = shifted((p2[0].astype(jnp.float32) + a_e[1]).astype(link), -1).astype(jnp.float32)
    b_l = shifted((p2[1].astype(jnp.float32) + a_l[1]).astype(link), 1).astype(jnp.float32)
    final_early = p3[0] + a_e[0] + b_e + jnp.where(at_top, a_l[1] + back, zero)
    final_late = p3[1] + a_l[0] + b_l
    final = jnp.stack([final_early, final_late])
    grad_keys = final[:, :, :kv_width].astype(jnp.bfloat16).reshape(keys.shape)
    grad_values = final[:, :, kv_width:].astype(jnp.bfloat16).reshape(values.shape)
    return (dq.reshape(query.shape), grad_keys, grad_values)


def solution(mesh):
    spec = P(AXIS, None, None, None)
    return jax.shard_map(
        on_device,
        mesh=mesh,
        in_specs=(spec, spec, spec, spec, P()),
        out_specs=(spec, spec, spec),
        check_vma=False,
    )
```
